512 devices in a mesh: space: 64 (over x, y_hi, z), chan: 8 (over y_lo, core).
Axes of the slice: x: 4, y: 8 (y_hi: 2, y_lo: 4; y = y_hi * 4 + y_lo), z: 8, core: 2. Of those that a mesh axis runs over, the one named last changes fastest.
Arguments:
- activation: float32 [64, 2, 512, 256], P('space', None, 'chan'), may hold values from -6 to 6
- weight: bfloat16 [3, 3, 3, 512, 512], P(None, None, None, 'chan'), may hold values from -0.0546875 to 0.0546875
- conv_bias: float32 [512], P('chan'), may hold values from -3 to 3
Outputs:
- output: float32 [64, 2, 512, 256], P('space', None, 'chan')
The draws below stay inside these ranges and needn't reach their ends.
All inputs are finite; a program needn't handle non-finite values.
Results may differ from the reference program's by a relative error of at most 0.0026.
Values may be sent and summed in bfloat16 or wider, within the bound.
No kernel may reach another device: no remote copies, remote signals or barrier semaphores. Data moves between devices by JAX's collectives and lax.ppermute only.
A program may use at most 64 MiB of HBM per device.

```python
import jax
import jax.numpy as jnp

C = 512
CX = 2
CY = 8
NZ = 32
PENCILS = 64
N_SPACE = 64


def block_scale(stream_key, dims, split, smallest, high):
    factor_of = 1.0
    for axis_at, parts in split:
        draws = jax.random.uniform(jax.random.fold_in(jax.random.fold_in(stream_key, 6), axis_at), (parts,), jnp.float32, smallest / len(split), high / len(split))
        factor_of = factor_of * jnp.repeat(jnp.exp(draws), dims[axis_at] // parts).reshape((-1,) + (1,) * (len(dims) - 1 - axis_at))
    return factor_of


def normal_values(rng, dims, scale, most, pieces=(), held_as=jnp.bfloat16):
    values = jax.random.normal(rng, dims, jnp.float32) * scale
    if len(pieces) > 0:
        values = block_scale(rng, dims, pieces, -0.22, 0.18) * values
    return jnp.clip(values, min=-most, max=most).astype(held_as)


def setup_inputs(seed: int = 0) -> dict:
    splits = jax.random.split(jax.random.key(seed), 4)
    return {
        "activation": normal_values(splits[0], (PENCILS, CX, C, CY * NZ), 1.0, 6.0, ((0, 64), (2, 8)), jnp.float32),
        "weight": normal_values(splits[1], (3, 3, 3, C, C), (27 * C) ** -0.5, 0.0546875, ((3, 8),)),
        "conv_bias": normal_values(splits[2], (C,), 0.5, 3.0, ((0, 8),), jnp.float32),
    }


def tap_sum(padded, kernel):
    size_x = padded.shape[0] - 2
    size_y = padded.shape[1] - 2
    size_z = padded.shape[2] - 2
    width_in = padded.shape[3]
    total = None
    for tap_x in range(3):
        for tap_y in range(3):
            columns = jnp.concatenate([padded[tap_x:tap_x + size_x, tap_y:tap_y + size_y, tap_z:tap_z + size_z, :] for tap_z in range(3)], axis=-1)
            columns = columns.reshape(-1, 3 * width_in)
            product = jnp.dot(columns, kernel[tap_x, tap_y].reshape(3 * width_in, -1), preferred_element_type=jnp.float32)
            total = product if total is None else total + product
    return total


def reference(activation, weight, conv_bias):
    groups_x = N_SPACE // 8
    lowered = activation.astype(jnp.bfloat16)
    lowered = lowered.reshape(N_SPACE, CX, C, CY, NZ).transpose(0, 1, 3, 4, 2)
    lowered = jnp.roll(lowered, -4, axis=0)
    volume = lowered.reshape(groups_x, 8, CX, CY, NZ, C).transpose(0, 2, 1, 3, 4, 5).reshape(groups_x * CX, 8 * CY, NZ, C)
    volume = jnp.concatenate([volume[-1:], volume, volume[:1]], axis=0)
    padded = jnp.pad(volume, ((0, 0), (1, 1), (1, 1), (0, 0)))
    kernel = weight.transpose(0, 1, 2, 4, 3)
    total = tap_sum(padded, kernel)
    before = total + conv_bias[None, :]
    result = jnp.maximum(before, 0.3 * before)
    result = result.reshape(groups_x, CX, 8, CY, NZ, C).transpose(0, 2, 1, 3, 4, 5)
    result = result.reshape(N_SPACE, CX, CY, NZ, C)
    result = jnp.roll(result, 4, axis=0).transpose(0, 1, 4, 2, 3)
    return result.reshape(N_SPACE, CX, C, CY * NZ)
```

```python
import jax
import jax.numpy as jnp
from jax import lax
from jax.sharding import PartitionSpec as P

CY = 8


negative_slope = 0.3


def shifted(value, axis, steps):
    count = lax.axis_size(axis)
    pairs = [(source, (source + steps) % count) for source in range(count)]
    return lax.ppermute(value, axis, pairs)


def haloed(own_block):
    stride_x = CY
    x_lo = shifted(own_block[-1:], "space", stride_x)
    x_hi = shifted(own_block[:1], "space", -stride_x)
    y_lo = shifted(own_block[:, -1:], "space", 1)
    y_hi = shifted(own_block[:, :1], "space", -1)
    c_ll = shifted(own_block[-1:, -1:], "space", stride_x + 1)
    c_lh = shifted(own_block[-1:, :1], "space", stride_x - 1)
    c_hl = shifted(own_block[:1, -1:], "space", 1 - stride_x)
    c_hh = shifted(own_block[:1, :1], "space", -stride_x - 1)
    lower_rim = jnp.concatenate([c_ll, y_lo, c_hl], axis=0)
    upper_rim = jnp.concatenate([c_lh, y_hi, c_hh], axis=0)
    place_y = (lax.axis_index("space") + 4) % 8
    lower_rim = jnp.where(place_y > 0, lower_rim, jnp.zeros_like(lower_rim))
    upper_rim = jnp.where(place_y < 7, upper_rim, jnp.zeros_like(upper_rim))
    widened = jnp.concatenate([x_lo, own_block, x_hi], axis=0)
    return jnp.concatenate([lower_rim, widened, upper_rim], axis=1)


def pad_depth(field):
    return jnp.pad(field, ((0, 0), (0, 0), (1, 1), (0, 0)))


def tap_sum(padded, kernel):
    size_x = padded.shape[0] - 2
    size_y = padded.shape[1] - 2
    size_z = padded.shape[2] - 2
    width_in = padded.shape[3]
    total = None
    for tap_x in range(3):
        for tap_y in range(3):
            columns = jnp.concatenate(
                [
                    padded[
                        tap_x : tap_x + size_x, tap_y : tap_y + size_y, tap_z : tap_z + size_z, :
                    ]
                    for tap_z in range(3)
                ],
                axis=-1,
            )
            columns = columns.reshape(-1, 3 * width_in)
            product = jnp.dot(
                columns,
                kernel[tap_x, tap_y].reshape(3 * width_in, -1),
                preferred_element_type=jnp.float32,
            )
            total = product if total is None else total + product
    return total


def body(activation, weight, conv_bias):
    size_x = activation.shape[1]
    width_in = activation.shape[2]
    size_y = CY
    size_z = activation.shape[3] // size_y
    own_block = (
        activation[0]
        .astype(jnp.bfloat16)
        .reshape(size_x, width_in, size_y, size_z)
        .transpose(0, 2, 3, 1)
    )
    kernel_all = weight.transpose(0, 1, 2, 4, 3)
    width_out = kernel_all.shape[4]
    gathered = lax.all_gather(own_block, "chan", axis=3, tiled=True)
    total = tap_sum(pad_depth(haloed(gathered)), kernel_all)
    before = total + conv_bias[None, :]
    result = jnp.maximum(before, negative_slope * before)
    result = result.reshape(size_x, size_y, size_z, width_out).transpose(0, 3, 1, 2)
    return result.reshape(1, size_x, width_out, size_y * size_z)


def solution(mesh):
    placed = (P("space", None, "chan", None), P(None, None, None, "chan", None), P("chan"))
    return jax.shard_map(
        body, mesh=mesh, in_specs=placed, out_specs=P("space", None, "chan", None), check_vma=False
    )
```

```python
import jax
import jax.numpy as jnp
from jax import lax
from jax.sharding import PartitionSpec as P

CY = 8


negative_slope = 0.3


def shifted(value, axis, steps):
    count = lax.axis_size(axis)
    pairs = [(source, (source + steps) % count) for source in range(count)]
    return lax.ppermute(value, axis, pairs)


def haloed(own_block):
    below = shifted(own_block[-1:], "space", 8)
    above = shifted(own_block[:1], "space", -8)
    widened = jnp.concatenate([below, own_block, above], axis=0)
    lower_from = shifted(widened[:, -1:], "space", 1)
    upper_from = shifted(widened[:, :1], "space", -1)
    place_y = (lax.axis_index("space") + 4) % 8
    lower_rim = jnp.where(place_y > 0, lower_from, jnp.zeros_like(lower_from))
    upper_rim = jnp.where(place_y < 7, upper_from, jnp.zeros_like(upper_from))
    return jnp.concatenate([lower_rim, widened, upper_rim], axis=1)


def pad_depth(field):
    return jnp.pad(field, ((0, 0), (0, 0), (1, 1), (0, 0)))


def tap_sum(padded, kernel):
    size_x = padded.shape[0] - 2
    size_y = padded.shape[1] - 2
    size_z = padded.shape[2] - 2
    width_in = padded.shape[3]
    total = None
    for tap_x in range(3):
        for tap_y in range(3):
            columns = jnp.concatenate(
                [
                    padded[
                        tap_x : tap_x + size_x, tap_y : tap_y + size_y, tap_z : tap_z + size_z, :
                    ]
                    for tap_z in range(3)
                ],
                axis=-1,
            )
            columns = columns.reshape(-1, 3 * width_in)
            product = jnp.dot(
                columns,
                kernel[tap_x, tap_y].reshape(3 * width_in, -1),
                preferred_element_type=jnp.float32,
            )
            total = product if total is None else total + product
    return total


def body(activation, weight, conv_bias):
    size_x = activation.shape[1]
    width_in = activation.shape[2]
    size_y = CY
    size_z = activation.shape[3] // size_y
    own_block = (
        activation[0]
        .astype(jnp.bfloat16)
        .reshape(size_x, width_in, size_y, size_z)
        .transpose(0, 2, 3, 1)
    )
    kernel_all = weight.transpose(0, 1, 2, 4, 3)
    width_out = kernel_all.shape[4]
    gathered = lax.all_gather(haloed(own_block), "chan", axis=3, tiled=True)
    total = tap_sum(pad_depth(gathered), kernel_all)
    before = total + conv_bias[None, :]
    result = jnp.maximum(before, negative_slope * before)
    result = result.reshape(size_x, size_y, size_z, width_out).transpose(0, 3, 1, 2)
    return result.reshape(1, size_x, width_out, size_y * size_z)


def solution(mesh):
    placed = (P("space", None, "chan", None), P(None, None, None, "chan", None), P("chan"))
    return jax.shard_map(
        body, mesh=mesh, in_specs=placed, out_specs=P("space", None, "chan", None), check_vma=False
    )
```

```python
import jax
import jax.numpy as jnp
from jax import lax
from jax.sharding import PartitionSpec as P

CY = 8


negative_slope = 0.3


def shifted(value, axis, steps):
    count = lax.axis_size(axis)
    width = lax.axis_size("chan")
    run_y = width // 2
    pairs = []
    for source in range(count):
        target = (source + steps) % count
        crosses = (source // CY) % 2 != (target // CY) % 2
        for lane in range(width):
            place, core = divmod(lane, 2)
            moved = ((place + run_y // 2) % run_y) * 2 + core if crosses else lane
            pairs.append((source * width + lane, target * width + moved))
    return lax.ppermute(value, (axis, "chan"), pairs)


def haloed(own_block):
    below = shifted(own_block[-1:], "space", 8)
    above = shifted(own_block[:1], "space", -8)
    widened = jnp.concatenate([below, own_block, above], axis=0)
    lower_from = shifted(widened[:, -1:], "space", 1)
    upper_from = shifted(widened[:, :1], "space", -1)
    place_y = (lax.axis_index("space") + 4) % 8
    lower_rim = jnp.where(place_y > 0, lower_from, jnp.zeros_like(lower_from))
    upper_rim = jnp.where(place_y < 7, upper_from, jnp.zeros_like(upper_from))
    return jnp.concatenate([lower_rim, widened, upper_rim], axis=1)


def pad_depth(field):
    return jnp.pad(field, ((0, 0), (0, 0), (1, 1), (0, 0)))


def tap_sum(padded, kernel):
    size_x = padded.shape[0] - 2
    size_y = padded.shape[1] - 2
    size_z = padded.shape[2] - 2
    width_in = padded.shape[3]
    total = None
    for tap_x in range(3):
        for tap_y in range(3):
            columns = jnp.concatenate(
                [
                    padded[
                        tap_x : tap_x + size_x, tap_y : tap_y + size_y, tap_z : tap_z + size_z, :
                    ]
                    for tap_z in range(3)
                ],
                axis=-1,
            )
            columns = columns.reshape(-1, 3 * width_in)
            product = jnp.dot(
                columns,
                kernel[tap_x, tap_y].reshape(3 * width_in, -1),
                preferred_element_type=jnp.float32,
            )
            total = product if total is None else total + product
    return total


def body(activation, weight, conv_bias):
    size_x = activation.shape[1]
    width_in = activation.shape[2]
    size_y = CY
    size_z = activation.shape[3] // size_y
    own_block = (
        activation[0]
        .astype(jnp.bfloat16)
        .reshape(size_x, width_in, size_y, size_z)
        .transpose(0, 2, 3, 1)
    )
    kernel_all = weight.transpose(0, 1, 2, 4, 3)
    width_out = kernel_all.shape[4]
    gathered = lax.all_gather(own_block, "chan", axis=3, tiled=True)
    total = tap_sum(pad_depth(haloed(gathered)), kernel_all)
    before = total + conv_bias[None, :]
    result = jnp.maximum(before, negative_slope * before)
    result = result.reshape(size_x, size_y, size_z, width_out).transpose(0, 3, 1, 2)
    return result.reshape(1, size_x, width_out, size_y * size_z)


def solution(mesh):
    placed = (P("space", None, "chan", None), P(None, None, None, "chan", None), P("chan"))
    return jax.shard_map(
        body, mesh=mesh, in_specs=placed, out_specs=P("space", None, "chan", None), check_vma=False
    )
```

```python
import jax
import jax.numpy as jnp
from jax import lax
from jax.sharding import PartitionSpec as P

CY = 8


negative_slope = 0.3


def shifted(value, axis, steps):
    count = lax.axis_size(axis)
    width = lax.axis_size("chan")
    run_y = width // 2
    pairs = []
    for source in range(count):
        target = (source + steps) % count
        crosses = (source // CY) % 2 != (target // CY) % 2
        for lane in range(width):
            place, core = divmod(lane, 2)
            moved = ((place + run_y // 2) % run_y) * 2 + core if crosses else lane
            pairs.append((source * width + lane, target * width + moved))
    return lax.ppermute(value, (axis, "chan"), pairs)


def haloed(own_block):
    below = shifted(own_block[:, -1:], "space", 8)
    above = shifted(own_block[:, :1], "space", -8)
    widened = jnp.concatenate([below, own_block, above], axis=1)
    lower_from = shifted(widened[:, :, -1:], "space", 1)
    upper_from = shifted(widened[:, :, :1], "space", -1)
    place_y = (lax.axis_index("space") + 4) % 8
    lower_rim = jnp.where(place_y > 0, lower_from, jnp.zeros_like(lower_from))
    upper_rim = jnp.where(place_y < 7, upper_from, jnp.zeros_like(upper_from))
    return jnp.concatenate([lower_rim, widened, upper_rim], axis=2)


def tap_sum(padded, weight):
    size_x = padded.shape[1] - 2
    size_y = padded.shape[2] - 2
    size_z = padded.shape[3] - 2
    width_in = padded.shape[0]
    total = None
    for tap_x in range(3):
        for tap_y in range(3):
            columns = jnp.concatenate(
                [
                    padded[
                        :, tap_x : tap_x + size_x, tap_y : tap_y + size_y, tap_z : tap_z + size_z
                    ]
                    for tap_z in range(3)
                ],
                axis=0,
            )
            columns = columns.reshape(3 * width_in, -1)
            taps = weight[tap_x, tap_y].transpose(1, 0, 2).reshape(-1, 3 * width_in)
            product = jnp.dot(taps, columns, preferred_element_type=jnp.float32)
            total = product if total is None else total + product
    return total


def body(activation, weight, conv_bias):
    size_x = activation.shape[1]
    width_in = activation.shape[2]
    size_y = CY
    size_z = activation.shape[3] // size_y
    own_block = activation[0].astype(jnp.bfloat16).transpose(1, 0, 2)
    gathered = lax.all_gather(own_block, "chan", axis=0, tiled=True)
    gathered = gathered.reshape(-1, size_x, size_y, size_z)
    padded = jnp.pad(haloed(gathered), ((0, 0), (0, 0), (0, 0), (1, 1)))
    total = tap_sum(padded, weight)
    width_out = total.shape[0]
    before = total + conv_bias[:, None]
    result = jnp.maximum(before, negative_slope * before)
    result = result.reshape(width_out, size_x, size_y * size_z).transpose(1, 0, 2)
    return result[None]


def solution(mesh):
    placed = (P("space", None, "chan", None), P(None, None, None, "chan", None), P("chan"))
    return jax.shard_map(
        body, mesh=mesh, in_specs=placed, out_specs=P("space", None, "chan", None), check_vma=False
    )
```

```python
import jax
import jax.numpy as jnp
from jax import lax
from jax.sharding import PartitionSpec as P

CY = 8


negative_slope = 0.3


def shifted(value, axis, steps):
    count = lax.axis_size(axis)
    width = lax.axis_size("chan")
    run_y = width // 2
    pairs = []
    for source in range(count):
        target = (source + steps) % count
        crosses = (source // CY) % 2 != (target // CY) % 2
        for lane in range(width):
            place, core = divmod(lane, 2)
            moved = ((place + run_y // 2) % run_y) * 2 + core if crosses else lane
            pairs.append((source * width + lane, target * width + moved))
    return lax.ppermute(value, (axis, "chan"), pairs)


def plain_shift(value, axis, steps):
    count = lax.axis_size(axis)
    return lax.ppermute(value, axis, [(source, (source + steps) % count) for source in range(count)])


def haloed(own_block, size_y):
    below = plain_shift(own_block[:, -1:], "space", 8)
    above = plain_shift(own_block[:, :1], "space", -8)
    gathered = lax.all_gather(own_block, "chan", axis=0, tiled=True)
    faces = lax.all_gather(jnp.concatenate([below, above], axis=1), "chan", axis=0, tiled=True)
    widened = jnp.concatenate([faces[:, :1], gathered, faces[:, 1:]], axis=1)
    widened = widened.reshape(widened.shape[0], widened.shape[1], size_y, -1)
    lower_from = shifted(widened[:, :, -1:], "space", 1)
    upper_from = shifted(widened[:, :, :1], "space", -1)
    place_y = (lax.axis_index("space") + 4) % 8
    lower_rim = jnp.where(place_y > 0, lower_from, jnp.zeros_like(lower_from))
    upper_rim = jnp.where(place_y < 7, upper_from, jnp.zeros_like(upper_from))
    return jnp.concatenate([lower_rim, widened, upper_rim], axis=2)


def tap_sum(padded, weight):
    size_x = padded.shape[1] - 2
    size_y = padded.shape[2] - 2
    size_z = padded.shape[3] - 2
    width_in = padded.shape[0]
    total = None
    for tap_x in range(3):
        for tap_y in range(3):
            columns = jnp.concatenate(
                [
                    padded[
                        :, tap_x : tap_x + size_x, tap_y : tap_y + size_y, tap_z : tap_z + size_z
                    ]
                    for tap_z in range(3)
                ],
                axis=0,
            )
            columns = columns.reshape(3 * width_in, -1)
            taps = weight[tap_x, tap_y].transpose(1, 0, 2).reshape(-1, 3 * width_in)
            product = jnp.dot(taps, columns, preferred_element_type=jnp.float32)
            total = product if total is None else total + product
    return total


def body(activation, weight, conv_bias):
    size_x = activation.shape[1]
    width_in = activation.shape[2]
    size_y = CY
    size_z = activation.shape[3] // size_y
    own_block = activation[0].astype(jnp.bfloat16).transpose(1, 0, 2)
    padded = jnp.pad(haloed(own_block, size_y), ((0, 0), (0, 0), (0, 0), (1, 1)))
    total = tap_sum(padded, weight)
    width_out = total.shape[0]
    before = total + conv_bias[:, None]
    result = jnp.maximum(before, negative_slope * before)
    result = result.reshape(width_out, size_x, size_y * size_z).transpose(1, 0, 2)
    return result[None]


def solution(mesh):
    placed = (P("space", None, "chan", None), P(None, None, None, "chan", None), P("chan"))
    return jax.shard_map(
        body, mesh=mesh, in_specs=placed, out_specs=P("space", None, "chan", None), check_vma=False
    )
```

```python
import jax
import jax.numpy as jnp
from jax import lax
from jax.sharding import PartitionSpec as P

CY = 8


negative_slope = 0.3


def shifted(value, axis, steps):
    count = lax.axis_size(axis)
    width = lax.axis_size("chan")
    run_y = width // 2
    pairs = []
    for source in range(count):
        target = (source + steps) % count
        crosses = (source // CY) % 2 != (target // CY) % 2
        for lane in range(width):
            place, core = divmod(lane, 2)
            moved = ((place + run_y // 2) % run_y) * 2 + core if crosses else lane
            pairs.append((source * width + lane, target * width + moved))
    return lax.ppermute(value, (axis, "chan"), pairs)


def haloed(own_block):
    below = shifted(own_block[:, -1:], "space", 8)
    above = shifted(own_block[:, :1], "space", -8)
    widened = jnp.concatenate([below, own_block, above], axis=1)
    lower_from = shifted(widened[:, :, -1:], "space", 1)
    upper_from = shifted(widened[:, :, :1], "space", -1)
    place_y = (lax.axis_index("space") + 4) % 8
    lower_rim = jnp.where(place_y > 0, lower_from, jnp.zeros_like(lower_from))
    upper_rim = jnp.where(place_y < 7, upper_from, jnp.zeros_like(upper_from))
    return jnp.concatenate([lower_rim, widened, upper_rim], axis=2)


def tap_sum(padded, weight):
    size_x = padded.shape[1] - 2
    size_y = padded.shape[2] - 2
    size_z = padded.shape[3] - 2
    width_in = padded.shape[0]
    total = None
    for tap_x in range(3):
        for tap_y in range(3):
            columns = jnp.concatenate(
                [
                    padded[
                        :, tap_x : tap_x + size_x, tap_y : tap_y + size_y, tap_z : tap_z + size_z
                    ]
                    for tap_z in range(3)
                ],
                axis=0,
            )
            columns = columns.reshape(3 * width_in, -1)
            taps = weight[tap_x, tap_y].transpose(1, 0, 2).reshape(-1, 3 * width_in)
            product = jnp.dot(taps, columns, preferred_element_type=jnp.float32)
            total = product if total is None else total + product
    return total


def body(activation, weight, conv_bias):
    size_x = activation.shape[1]
    width_in = activation.shape[2]
    size_y = CY
    size_z = activation.shape[3] // size_y
    own_block = activation[0].astype(jnp.bfloat16).transpose(1, 0, 2)
    gathered = lax.all_gather(own_block, "chan", axis=0, tiled=True)
    gathered = gathered.reshape(-1, size_x, size_y, size_z)
    total = lax.conv_general_dilated(
        haloed(gathered)[None],
        weight,
        window_strides=(1, 1, 1),
        padding=((0, 0), (0, 0), (1, 1)),
        dimension_numbers=("NCDHW", "DHWOI", "NCDHW"),
        preferred_element_type=jnp.float32,
    )[0]
    width_out = total.shape[0]
    total = total.reshape(width_out, -1)
    before = total + conv_bias[:, None]
    result = jnp.maximum(before, negative_slope * before)
    result = result.reshape(width_out, size_x, size_y * size_z).transpose(1, 0, 2)
    return result[None]


def solution(mesh):
    placed = (P("space", None, "chan", None), P(None, None, None, "chan", None), P("chan"))
    return jax.shard_map(
        body, mesh=mesh, in_specs=placed, out_specs=P("space", None, "chan", None), check_vma=False
    )
```

```python
import jax
import jax.numpy as jnp
from jax import lax
from jax.sharding import PartitionSpec as P

CY = 8


negative_slope = 0.3


def shifted(value, axis, steps):
    count = lax.axis_size(axis)
    width = lax.axis_size("chan")
    run_y = width // 2
    pairs = []
    for source in range(count):
        target = (source + steps) % count
        crosses = (source // CY) % 2 != (target // CY) % 2
        for lane in range(width):
            place, core = divmod(lane, 2)
            moved = ((place + run_y // 2) % run_y) * 2 + core if crosses else lane
            pairs.append((source * width + lane, target * width + moved))
    return lax.ppermute(value, (axis, "chan"), pairs)


def conv(field, taps, padding):
    return lax.conv_general_dilated(
        field[None],
        taps,
        window_strides=(1, 1, 1),
        padding=padding,
        dimension_numbers=("NCDHW", "DHWOI", "NCDHW"),
        preferred_element_type=jnp.float32,
    )[0]


def body(activation, weight, conv_bias):
    size_x = activation.shape[1]
    size_y = CY
    size_z = activation.shape[3] // size_y
    own_block = activation[0].astype(jnp.bfloat16).transpose(1, 0, 2)
    gathered = lax.all_gather(own_block, "chan", axis=0, tiled=True)
    gathered = gathered.reshape(-1, size_x, size_y, size_z)
    below = shifted(gathered[:, -1:], "space", 8)
    above = shifted(gathered[:, :1], "space", -8)
    own_part = conv(gathered, weight, ((1, 1), (1, 1), (1, 1)))
    face_part = jnp.concatenate(
        [
            conv(below, weight[:1], ((0, 0), (1, 1), (1, 1))),
            conv(above, weight[2:], ((0, 0), (1, 1), (1, 1))),
        ],
        axis=1,
    )
    widened = jnp.concatenate([below, gathered, above], axis=1)
    lower_from = shifted(widened[:, :, -1:], "space", 1)
    upper_from = shifted(widened[:, :, :1], "space", -1)
    place_y = (lax.axis_index("space") + 4) % 8
    lower_rim = jnp.where(place_y > 0, lower_from, jnp.zeros_like(lower_from))
    upper_rim = jnp.where(place_y < 7, upper_from, jnp.zeros_like(upper_from))
    lower_part = conv(lower_rim, weight[:, :1], ((0, 0), (0, 0), (1, 1)))
    upper_part = conv(upper_rim, weight[:, 2:], ((0, 0), (0, 0), (1, 1)))
    width_out = own_part.shape[0]
    middle = jnp.zeros((width_out, size_x, size_y - 2, size_z), jnp.float32)
    rim_part = jnp.concatenate([lower_part, middle, upper_part], axis=2)
    total = (own_part + face_part + rim_part).reshape(width_out, -1)
    before = total + conv_bias[:, None]
    result = jnp.maximum(before, negative_slope * before)
    result = result.reshape(width_out, size_x, size_y * size_z).transpose(1, 0, 2)
    return result[None]


def solution(mesh):
    placed = (P("space", None, "chan", None), P(None, None, None, "chan", None), P("chan"))
    return jax.shard_map(
        body, mesh=mesh, in_specs=placed, out_specs=P("space", None, "chan", None), check_vma=False
    )
```

```python
import jax
import jax.numpy as jnp
from jax import lax
from jax.sharding import PartitionSpec as P

CY = 8


negative_slope = 0.3


def faces_from(lower_source, upper_source, axis, steps):
    count = lax.axis_size(axis)
    width = lax.axis_size("chan")
    run_y = width // 2
    pairs = []
    for source in range(count):
        for lane in range(width):
            place, core = divmod(lane, 2)
            target = (source + (steps if core == 0 else -steps)) % count
            crosses = (source // CY) % 2 != (target // CY) % 2
            moved = ((place + run_y // 2) % run_y) * 2 + core if crosses else lane
            pairs.append((source * width + lane, target * width + moved))
    on_first = lax.axis_index("chan") % 2 == 0
    sent = jnp.where(on_first, lower_source, upper_source)
    got = lax.ppermute(sent, (axis, "chan"), pairs)
    swapped = lax.ppermute(got, "chan", [(lane, lane ^ 1) for lane in range(width)])
    return jnp.where(on_first, got, swapped), jnp.where(on_first, swapped, got)


def conv(field, taps, padding):
    return lax.conv_general_dilated(
        field[None],
        taps,
        window_strides=(1, 1, 1),
        padding=padding,
        dimension_numbers=("NCDHW", "DHWOI", "NCDHW"),
        preferred_element_type=jnp.float32,
    )[0]


def body(activation, weight, conv_bias):
    size_x = activation.shape[1]
    size_y = CY
    size_z = activation.shape[3] // size_y
    own_block = activation[0].astype(jnp.bfloat16).transpose(1, 0, 2)
    gathered = lax.all_gather(own_block, "chan", axis=0, tiled=True)
    gathered = gathered.reshape(-1, size_x, size_y, size_z)
    below, above = faces_from(gathered[:, -1:], gathered[:, :1], "space", 8)
    own_part = conv(gathered, weight, ((1, 1), (1, 1), (1, 1)))
    face_part = jnp.concatenate(
        [
            conv(below, weight[:1], ((0, 0), (1, 1), (1, 1))),
            conv(above, weight[2:], ((0, 0), (1, 1), (1, 1))),
        ],
        axis=1,
    )
    widened = jnp.concatenate([below, gathered, above], axis=1)
    lower_from, upper_from = faces_from(widened[:, :, -1:], widened[:, :, :1], "space", 1)
    place_y = (lax.axis_index("space") + 4) % 8
    lower_rim = jnp.where(place_y > 0, lower_from, jnp.zeros_like(lower_from))
    upper_rim = jnp.where(place_y < 7, upper_from, jnp.zeros_like(upper_from))
    lower_part = conv(lower_rim, weight[:, :1], ((0, 0), (0, 0), (1, 1)))
    upper_part = conv(upper_rim, weight[:, 2:], ((0, 0), (0, 0), (1, 1)))
    width_out = own_part.shape[0]
    middle = jnp.zeros((width_out, size_x, size_y - 2, size_z), jnp.float32)
    rim_part = jnp.concatenate([lower_part, middle, upper_part], axis=2)
    total = (own_part + face_part + rim_part).reshape(width_out, -1)
    before = total + conv_bias[:, None]
    result = jnp.maximum(before, negative_slope * before)
    result = result.reshape(width_out, size_x, size_y * size_z).transpose(1, 0, 2)
    return result[None]


def solution(mesh):
    placed = (P("space", None, "chan", None), P(None, None, None, "chan", None), P("chan"))
    return jax.shard_map(
        body, mesh=mesh, in_specs=placed, out_specs=P("space", None, "chan", None), check_vma=False
    )
```

```python
import jax
import jax.numpy as jnp
from jax import lax
from jax.sharding import PartitionSpec as P

CY = 8


negative_slope = 0.3


def faces_from(lower_source, upper_source, axis, steps, cover=None):
    count = lax.axis_size(axis)
    width = lax.axis_size("chan")
    run_y = width // 2
    pairs = []
    for source in range(count):
        for lane in range(width):
            place, core = divmod(lane, 2)
            target = (source + (steps if core == 0 else -steps)) % count
            crosses = (source // CY) % 2 != (target // CY) % 2
            moved = ((place + run_y // 2) % run_y) * 2 + core if crosses else lane
            pairs.append((source * width + lane, target * width + moved))
    on_first = lax.axis_index("chan") % 2 == 0
    sent = jnp.where(on_first, lower_source, upper_source)
    got = lax.ppermute(sent, (axis, "chan"), pairs)
    if cover is not None:
        got, cover = lax.optimization_barrier((got, cover))
    swapped = lax.ppermute(got, "chan", [(lane, lane ^ 1) for lane in range(width)])
    return jnp.where(on_first, got, swapped), jnp.where(on_first, swapped, got), cover


def conv(field, taps, padding):
    return lax.conv_general_dilated(
        field[None],
        taps,
        window_strides=(1, 1, 1),
        padding=padding,
        dimension_numbers=("NCDHW", "DHWOI", "NCDHW"),
        preferred_element_type=jnp.float32,
    )[0]


def body(activation, weight, conv_bias):
    size_x = activation.shape[1]
    size_y = CY
    size_z = activation.shape[3] // size_y
    own_block = activation[0].astype(jnp.bfloat16).transpose(1, 0, 2)
    gathered = lax.all_gather(own_block, "chan", axis=0, tiled=True)
    gathered = gathered.reshape(-1, size_x, size_y, size_z)
    own_part = conv(gathered, weight, ((1, 1), (1, 1), (1, 1)))
    below, above, own_part = faces_from(gathered[:, -1:], gathered[:, :1], "space", 8, own_part)
    face_part = jnp.concatenate(
        [
            conv(below, weight[:1], ((0, 0), (1, 1), (1, 1))),
            conv(above, weight[2:], ((0, 0), (1, 1), (1, 1))),
        ],
        axis=1,
    )
    widened = jnp.concatenate([below, gathered, above], axis=1)
    lower_from, upper_from, _ = faces_from(widened[:, :, -1:], widened[:, :, :1], "space", 1)
    place_y = (lax.axis_index("space") + 4) % 8
    lower_rim = jnp.where(place_y > 0, lower_from, jnp.zeros_like(lower_from))
    upper_rim = jnp.where(place_y < 7, upper_from, jnp.zeros_like(upper_from))
    lower_part = conv(lower_rim, weight[:, :1], ((0, 0), (0, 0), (1, 1)))
    upper_part = conv(upper_rim, weight[:, 2:], ((0, 0), (0, 0), (1, 1)))
    width_out = own_part.shape[0]
    middle = jnp.zeros((width_out, size_x, size_y - 2, size_z), jnp.float32)
    rim_part = jnp.concatenate([lower_part, middle, upper_part], axis=2)
    total = (own_part + face_part + rim_part).reshape(width_out, -1)
    before = total + conv_bias[:, None]
    result = jnp.maximum(before, negative_slope * before)
    result = result.reshape(width_out, size_x, size_y * size_z).transpose(1, 0, 2)
    return result[None]


def solution(mesh):
    placed = (P("space", None, "chan", None), P(None, None, None, "chan", None), P("chan"))
    return jax.shard_map(
        body, mesh=mesh, in_specs=placed, out_specs=P("space", None, "chan", None), check_vma=False
    )
```

```python
import jax
import jax.numpy as jnp
from jax import lax
from jax.sharding import PartitionSpec as P

CY = 8


negative_slope = 0.3


def cross(lower_source, upper_source, axis, steps):
    count = lax.axis_size(axis)
    width = lax.axis_size("chan")
    run_y = width // 2
    pairs = []
    for source in range(count):
        for lane in range(width):
            place, core = divmod(lane, 2)
            target = (source + (steps if core == 0 else -steps)) % count
            crosses = (source // CY) % 2 != (target // CY) % 2
            moved = ((place + run_y // 2) % run_y) * 2 + core if crosses else lane
            pairs.append((source * width + lane, target * width + moved))
    on_first = lax.axis_index("chan") % 2 == 0
    sent = jnp.where(on_first, lower_source, upper_source)
    return lax.ppermute(sent, (axis, "chan"), pairs)


def swap(got):
    width = lax.axis_size("chan")
    on_first = lax.axis_index("chan") % 2 == 0
    swapped = lax.ppermute(got, "chan", [(lane, lane ^ 1) for lane in range(width)])
    return jnp.where(on_first, got, swapped), jnp.where(on_first, swapped, got)


def conv(field, taps, padding):
    return lax.conv_general_dilated(
        field[None],
        taps,
        window_strides=(1, 1, 1),
        padding=padding,
        dimension_numbers=("NCDHW", "DHWOI", "NCDHW"),
        preferred_element_type=jnp.float32,
    )[0]


def body(activation, weight, conv_bias):
    size_x = activation.shape[1]
    size_y = CY
    size_z = activation.shape[3] // size_y
    own_block = activation[0].astype(jnp.bfloat16).transpose(1, 0, 2)
    gathered = lax.all_gather(own_block, "chan", axis=0, tiled=True)
    gathered = gathered.reshape(-1, size_x, size_y, size_z)
    own_part = conv(gathered, weight, ((1, 1), (1, 1), (1, 1)))
    got_x = cross(gathered[:, -1:], gathered[:, :1], "space", 8)
    got_y = cross(gathered[:, :, -1:], gathered[:, :, :1], "space", 1)
    got_x, got_y, own_part = lax.optimization_barrier((got_x, got_y, own_part))
    below, above = swap(got_x)
    lower_row, upper_row = swap(got_y)
    place_y = (lax.axis_index("space") + 4) % 8
    lower_row = jnp.where(place_y > 0, lower_row, jnp.zeros_like(lower_row))
    upper_row = jnp.where(place_y < 7, upper_row, jnp.zeros_like(upper_row))
    got_corners = cross(
        jnp.concatenate([lower_row[:, -1:], upper_row[:, -1:]], axis=2),
        jnp.concatenate([lower_row[:, :1], upper_row[:, :1]], axis=2),
        "space",
        8,
    )
    face_part = jnp.concatenate(
        [
            conv(below, weight[:1], ((0, 0), (1, 1), (1, 1))),
            conv(above, weight[2:], ((0, 0), (1, 1), (1, 1))),
        ],
        axis=1,
    )
    got_corners, face_part = lax.optimization_barrier((got_corners, face_part))
    corner_lo, corner_hi = swap(got_corners)
    lower_rim = jnp.concatenate([corner_lo[:, :, :1], lower_row, corner_hi[:, :, :1]], axis=1)
    upper_rim = jnp.concatenate([corner_lo[:, :, 1:], upper_row, corner_hi[:, :, 1:]], axis=1)
    lower_part = conv(lower_rim, weight[:, :1], ((0, 0), (0, 0), (1, 1)))
    upper_part = conv(upper_rim, weight[:, 2:], ((0, 0), (0, 0), (1, 1)))
    width_out = own_part.shape[0]
    middle = jnp.zeros((width_out, size_x, size_y - 2, size_z), jnp.float32)
    rim_part = jnp.concatenate([lower_part, middle, upper_part], axis=2)
    total = (own_part + face_part + rim_part).reshape(width_out, -1)
    before = total + conv_bias[:, None]
    result = jnp.maximum(before, negative_slope * before)
    result = result.reshape(width_out, size_x, size_y * size_z).transpose(1, 0, 2)
    return result[None]


def solution(mesh):
    placed = (P("space", None, "chan", None), P(None, None, None, "chan", None), P("chan"))
    return jax.shard_map(
        body, mesh=mesh, in_specs=placed, out_specs=P("space", None, "chan", None), check_vma=False
    )
```

```python
import jax
import jax.numpy as jnp
from jax import lax
from jax.sharding import PartitionSpec as P

CY = 8


negative_slope = 0.3


def cross(lower_source, upper_source, axis, steps):
    count = lax.axis_size(axis)
    width = lax.axis_size("chan")
    run_y = width // 2
    pairs = []
    for source in range(count):
        for lane in range(width):
            place, core = divmod(lane, 2)
            target = (source + (steps if core == 0 else -steps)) % count
            crosses = (source // CY) % 2 != (target // CY) % 2
            moved = ((place + run_y // 2) % run_y) * 2 + core if crosses else lane
            pairs.append((source * width + lane, target * width + moved))
    on_first = lax.axis_index("chan") % 2 == 0
    sent = jnp.where(on_first, lower_source, upper_source)
    return lax.ppermute(sent, (axis, "chan"), pairs)


def swap(got):
    width = lax.axis_size("chan")
    on_first = lax.axis_index("chan") % 2 == 0
    swapped = lax.ppermute(got, "chan", [(lane, lane ^ 1) for lane in range(width)])
    return jnp.where(on_first, got, swapped), jnp.where(on_first, swapped, got)


def conv(field, taps, padding):
    return lax.conv_general_dilated(
        field[None],
        taps,
        window_strides=(1, 1, 1),
        padding=padding,
        dimension_numbers=("NCDHW", "DHWOI", "NCDHW"),
        preferred_element_type=jnp.float32,
    )[0]


def body(activation, weight, conv_bias):
    size_x = activation.shape[1]
    size_y = CY
    size_z = activation.shape[3] // size_y
    own_block = activation[0].astype(jnp.bfloat16).transpose(1, 0, 2)
    gathered = lax.all_gather(own_block, "chan", axis=0, tiled=True)
    gathered = gathered.reshape(-1, size_x, size_y, size_z)
    own_part = conv(gathered, weight, ((1, 1), (1, 1), (1, 1)))
    width_in = gathered.shape[0]
    got = [
        cross(gathered[:, -1:], gathered[:, :1], "space", CY),
        cross(gathered[:, :, -1:], gathered[:, :, :1], "space", 1),
        cross(gathered[:, -1:, -1:], gathered[:, :1, :1], "space", CY + 1),
        cross(gathered[:, -1:, :1], gathered[:, :1, -1:], "space", CY - 1),
    ]
    got, own_part = lax.optimization_barrier((got, own_part))
    sizes = [piece[0].size for piece in got]
    joined = jnp.concatenate([piece.reshape(width_in, -1) for piece in got], axis=1)
    lower_all, upper_all = swap(joined)
    offsets = [sum(sizes[:k]) for k in range(len(sizes) + 1)]

    def piece(joined_half, k):
        return joined_half[:, offsets[k] : offsets[k + 1]].reshape(got[k].shape)

    below, above = piece(lower_all, 0), piece(upper_all, 0)
    lower_row, upper_row = piece(lower_all, 1), piece(upper_all, 1)
    corner_ll, corner_hh = piece(lower_all, 2), piece(upper_all, 2)
    corner_lh, corner_hl = piece(lower_all, 3), piece(upper_all, 3)
    face_part = jnp.concatenate(
        [
            conv(below, weight[:1], ((0, 0), (1, 1), (1, 1))),
            conv(above, weight[2:], ((0, 0), (1, 1), (1, 1))),
        ],
        axis=1,
    )
    place_y = (lax.axis_index("space") + 4) % 8
    lower_rim = jnp.concatenate([corner_ll, lower_row, corner_hl], axis=1)
    upper_rim = jnp.concatenate([corner_lh, upper_row, corner_hh], axis=1)
    lower_rim = jnp.where(place_y > 0, lower_rim, jnp.zeros_like(lower_rim))
    upper_rim = jnp.where(place_y < 7, upper_rim, jnp.zeros_like(upper_rim))
    lower_part = conv(lower_rim, weight[:, :1], ((0, 0), (0, 0), (1, 1)))
    upper_part = conv(upper_rim, weight[:, 2:], ((0, 0), (0, 0), (1, 1)))
    width_out = own_part.shape[0]
    middle = jnp.zeros((width_out, size_x, size_y - 2, size_z), jnp.float32)
    rim_part = jnp.concatenate([lower_part, middle, upper_part], axis=2)
    total = (own_part + face_part + rim_part).reshape(width_out, -1)
    before = total + conv_bias[:, None]
    result = jnp.maximum(before, negative_slope * before)
    result = result.reshape(width_out, size_x, size_y * size_z).transpose(1, 0, 2)
    return result[None]


def solution(mesh):
    placed = (P("space", None, "chan", None), P(None, None, None, "chan", None), P("chan"))
    return jax.shard_map(
        body, mesh=mesh, in_specs=placed, out_specs=P("space", None, "chan", None), check_vma=False
    )
```

```python
import jax
import jax.numpy as jnp
from jax import lax
from jax.sharding import PartitionSpec as P

CY = 8


negative_slope = 0.3


def cross(lower_source, upper_source, axis, steps):
    count = lax.axis_size(axis)
    width = lax.axis_size("chan")
    run_y = width // 2
    pairs = []
    for source in range(count):
        for lane in range(width):
            place, core = divmod(lane, 2)
            target = (source + (steps if core == 0 else -steps)) % count
            crosses = (source // CY) % 2 != (target // CY) % 2
            moved = ((place + run_y // 2) % run_y) * 2 + core if crosses else lane
            pairs.append((source * width + lane, target * width + moved))
    on_first = lax.axis_index("chan") % 2 == 0
    sent = jnp.where(on_first, lower_source, upper_source)
    return lax.ppermute(sent, (axis, "chan"), pairs)


def swap(got):
    width = lax.axis_size("chan")
    on_first = lax.axis_index("chan") % 2 == 0
    swapped = lax.ppermute(got, "chan", [(lane, lane ^ 1) for lane in range(width)])
    return jnp.where(on_first, got, swapped), jnp.where(on_first, swapped, got)


def conv(field, taps, padding):
    return lax.conv_general_dilated(
        field[None],
        taps,
        window_strides=(1, 1, 1),
        padding=padding,
        dimension_numbers=("NCDHW", "DHWOI", "NCDHW"),
        preferred_element_type=jnp.float32,
    )[0]


def body(activation, weight, conv_bias):
    size_x = activation.shape[1]
    size_y = CY
    size_z = activation.shape[3] // size_y
    own_block = activation[0].astype(jnp.bfloat16).transpose(1, 0, 2)
    gathered = lax.all_gather(own_block, "chan", axis=0, tiled=True)
    gathered = gathered.reshape(-1, size_x, size_y, size_z)
    own_part = conv(gathered, weight, ((1, 1), (1, 1), (1, 1)))
    width_in = gathered.shape[0]
    got = [
        cross(gathered[:, -1:], gathered[:, :1], "space", CY),
        cross(gathered[:, :, -1:], gathered[:, :, :1], "space", 1),
    ]
    corners_from, own_part = lax.optimization_barrier((gathered[:, ::size_x - 1, ::size_y - 1], own_part))
    got += [
        cross(corners_from[:, 1:, 1:], corners_from[:, :1, :1], "space", CY + 1),
        cross(corners_from[:, 1:, :1], corners_from[:, :1, 1:], "space", CY - 1),
    ]
    got, own_part = lax.optimization_barrier((got, own_part))
    sizes = [piece[0].size for piece in got]
    joined = jnp.concatenate([piece.reshape(width_in, -1) for piece in got], axis=1)
    lower_all, upper_all = swap(joined)
    offsets = [sum(sizes[:k]) for k in range(len(sizes) + 1)]

    def piece(joined_half, k):
        return joined_half[:, offsets[k] : offsets[k + 1]].reshape(got[k].shape)

    below, above = piece(lower_all, 0), piece(upper_all, 0)
    lower_row, upper_row = piece(lower_all, 1), piece(upper_all, 1)
    corner_ll, corner_hh = piece(lower_all, 2), piece(upper_all, 2)
    corner_lh, corner_hl = piece(lower_all, 3), piece(upper_all, 3)
    face_part = jnp.concatenate(
        [
            conv(below, weight[:1], ((0, 0), (1, 1), (1, 1))),
            conv(above, weight[2:], ((0, 0), (1, 1), (1, 1))),
        ],
        axis=1,
    )
    place_y = (lax.axis_index("space") + 4) % 8
    lower_rim = jnp.concatenate([corner_ll, lower_row, corner_hl], axis=1)
    upper_rim = jnp.concatenate([corner_lh, upper_row, corner_hh], axis=1)
    lower_rim = jnp.where(place_y > 0, lower_rim, jnp.zeros_like(lower_rim))
    upper_rim = jnp.where(place_y < 7, upper_rim, jnp.zeros_like(upper_rim))
    lower_part = conv(lower_rim, weight[:, :1], ((0, 0), (0, 0), (1, 1)))
    upper_part = conv(upper_rim, weight[:, 2:], ((0, 0), (0, 0), (1, 1)))
    width_out = own_part.shape[0]
    middle = jnp.zeros((width_out, size_x, size_y - 2, size_z), jnp.float32)
    rim_part = jnp.concatenate([lower_part, middle, upper_part], axis=2)
    total = (own_part + face_part + rim_part).reshape(width_out, -1)
    before = total + conv_bias[:, None]
    result = jnp.maximum(before, negative_slope * before)
    result = result.reshape(width_out, size_x, size_y * size_z).transpose(1, 0, 2)
    return result[None]


def solution(mesh):
    placed = (P("space", None, "chan", None), P(None, None, None, "chan", None), P("chan"))
    return jax.shard_map(
        body, mesh=mesh, in_specs=placed, out_specs=P("space", None, "chan", None), check_vma=False
    )
```

```python
import jax
import jax.numpy as jnp
from jax import lax
from jax.sharding import PartitionSpec as P

CY = 8


negative_slope = 0.3


def cross(lower_source, upper_source, axis, steps):
    count = lax.axis_size(axis)
    width = lax.axis_size("chan")
    run_y = width // 2
    pairs = []
    for source in range(count):
        for lane in range(width):
            place, core = divmod(lane, 2)
            target = (source + (steps if core == 0 else -steps)) % count
            crosses = (source // CY) % 2 != (target // CY) % 2
            moved = ((place + run_y // 2) % run_y) * 2 + core if crosses else lane
            pairs.append((source * width + lane, target * width + moved))
    on_first = lax.axis_index("chan") % 2 == 0
    sent = jnp.where(on_first, lower_source, upper_source)
    return lax.ppermute(sent, (axis, "chan"), pairs)


def swap(got):
    width = lax.axis_size("chan")
    on_first = lax.axis_index("chan") % 2 == 0
    swapped = lax.ppermute(got, "chan", [(lane, lane ^ 1) for lane in range(width)])
    return jnp.where(on_first, got, swapped), jnp.where(on_first, swapped, got)


def conv(field, taps, padding):
    return lax.conv_general_dilated(
        field[None],
        taps,
        window_strides=(1, 1, 1),
        padding=padding,
        dimension_numbers=("NCDHW", "DHWOI", "NCDHW"),
        preferred_element_type=jnp.float32,
    )[0]


def body(activation, weight, conv_bias):
    size_x = activation.shape[1]
    size_y = CY
    size_z = activation.shape[3] // size_y
    own_block = activation[0].astype(jnp.bfloat16).transpose(1, 0, 2)
    gathered = lax.all_gather(own_block, "chan", axis=0, tiled=True)
    gathered = gathered.reshape(-1, size_x, size_y, size_z)
    own_part = conv(gathered, weight, ((1, 1), (1, 1), (1, 1)))
    width_in = gathered.shape[0]
    got = [
        cross(gathered[:, -1:], gathered[:, :1], "space", CY),
        cross(gathered[:, :, -1:], gathered[:, :, :1], "space", 1),
    ]
    corners_from, own_part = lax.optimization_barrier((gathered[:, ::size_x - 1, ::size_y - 1], own_part))
    got += [
        cross(corners_from[:, 1:, 1:], corners_from[:, :1, :1], "space", CY + 1),
        cross(corners_from[:, 1:, :1], corners_from[:, :1, 1:], "space", CY - 1),
    ]
    got, own_part = lax.optimization_barrier((got, own_part))
    sizes = [piece[0].size for piece in got]
    offsets = [sum(sizes[:k]) for k in range(len(sizes) + 1)]
    mine = jnp.concatenate([piece.reshape(width_in, -1) for piece in got], axis=1)
    width = lax.axis_size("chan")
    parity = lax.axis_index("chan") % 2
    place_y = (lax.axis_index("space") + 4) % 8

    def halo_part(joined, side):
        face, row, corner_a, corner_b = (
            joined[:, offsets[k] : offsets[k + 1]].reshape(got[k].shape) for k in range(4)
        )
        width_out = weight.shape[3]
        zeros_rim = jnp.zeros((width_in, size_x + 2, 1, size_z), joined.dtype)
        row_rim = lax.dynamic_update_slice(zeros_rim, row, (0, 1, 0, 0))
        row_rim = lax.dynamic_update_slice(row_rim, corner_a, (0, 3 * side, 0, 0))
        corner_rim = lax.dynamic_update_slice(zeros_rim, corner_b, (0, 3 * side, 0, 0))
        face_taps = lax.dynamic_slice_in_dim(weight, 2 * side, 1, axis=0)
        row_taps = lax.dynamic_slice_in_dim(weight, 2 * side, 1, axis=1)
        corner_taps = lax.dynamic_slice_in_dim(weight, 2 - 2 * side, 1, axis=1)
        face_out = conv(face, face_taps, ((0, 0), (1, 1), (1, 1)))
        row_out = conv(row_rim, row_taps, ((0, 0), (0, 0), (1, 1)))
        corner_out = conv(corner_rim, corner_taps, ((0, 0), (0, 0), (1, 1)))
        row_valid = jnp.where(side == 0, place_y > 0, place_y < 7)
        corner_valid = jnp.where(side == 0, place_y < 7, place_y > 0)
        row_out = jnp.where(row_valid, row_out, jnp.zeros_like(row_out))
        corner_out = jnp.where(corner_valid, corner_out, jnp.zeros_like(corner_out))
        zeros_out = jnp.zeros((width_out, size_x, size_y, size_z), jnp.float32)
        part = lax.dynamic_update_slice(zeros_out, face_out, (0, side, 0, 0))
        part = part + lax.dynamic_update_slice(zeros_out, row_out, (0, 0, (size_y - 1) * side, 0))
        return part + lax.dynamic_update_slice(zeros_out, corner_out, (0, 0, (size_y - 1) * (1 - side), 0))

    other = lax.ppermute(mine, "chan", [(lane, lane ^ 1) for lane in range(width)])
    mine_part = halo_part(mine, parity)
    other, mine_part = lax.optimization_barrier((other, mine_part))
    own_part = own_part + mine_part + halo_part(other, 1 - parity)
    width_out = own_part.shape[0]
    total = own_part.reshape(width_out, -1)
    before = total + conv_bias[:, None]
    result = jnp.maximum(before, negative_slope * before)
    result = result.reshape(width_out, size_x, size_y * size_z).transpose(1, 0, 2)
    return result[None]


def solution(mesh):
    placed = (P("space", None, "chan", None), P(None, None, None, "chan", None), P("chan"))
    return jax.shard_map(
        body, mesh=mesh, in_specs=placed, out_specs=P("space", None, "chan", None), check_vma=False
    )
```

```python
import jax
import jax.numpy as jnp
from jax import lax
from jax.sharding import PartitionSpec as P

CY = 8


negative_slope = 0.3


def cross(lower_source, upper_source, axis, steps):
    count = lax.axis_size(axis)
    width = lax.axis_size("chan")
    run_y = width // 2
    pairs = []
    for source in range(count):
        for lane in range(width):
            place, core = divmod(lane, 2)
            target = (source + (steps if core == 0 else -steps)) % count
            crosses = (source // CY) % 2 != (target // CY) % 2
            moved = ((place + run_y // 2) % run_y) * 2 + core if crosses else lane
            pairs.append((source * width + lane, target * width + moved))
    on_first = lax.axis_index("chan") % 2 == 0
    sent = jnp.where(on_first, lower_source, upper_source)
    return lax.ppermute(sent, (axis, "chan"), pairs)


def swap(got):
    width = lax.axis_size("chan")
    on_first = lax.axis_index("chan") % 2 == 0
    swapped = lax.ppermute(got, "chan", [(lane, lane ^ 1) for lane in range(width)])
    return jnp.where(on_first, got, swapped), jnp.where(on_first, swapped, got)


def conv(field, taps, padding):
    return lax.conv_general_dilated(
        field[None],
        taps,
        window_strides=(1, 1, 1),
        padding=padding,
        dimension_numbers=("NCDHW", "DHWOI", "NCDHW"),
        preferred_element_type=jnp.float32,
    )[0]


def body(activation, weight, conv_bias):
    size_x = activation.shape[1]
    size_y = CY
    size_z = activation.shape[3] // size_y
    width = lax.axis_size("chan")
    own_block = activation[0].astype(jnp.bfloat16).reshape(-1, activation.shape[3])
    gathered = lax.all_gather(own_block, "chan", axis=0, tiled=True)
    gathered = gathered.reshape(width, size_x, -1, activation.shape[3]).transpose(0, 2, 1, 3)
    gathered = gathered.reshape(-1, size_x, size_y, size_z)
    own_part = conv(gathered, weight, ((1, 1), (1, 1), (1, 1)))
    width_in = gathered.shape[0]
    got = [
        cross(gathered[:, -1:], gathered[:, :1], "space", CY),
        cross(gathered[:, :, -1:], gathered[:, :, :1], "space", 1),
    ]
    corners_from, own_part = lax.optimization_barrier((gathered[:, ::size_x - 1, ::size_y - 1], own_part))
    got += [
        cross(corners_from[:, 1:, 1:], corners_from[:, :1, :1], "space", CY + 1),
        cross(corners_from[:, 1:, :1], corners_from[:, :1, 1:], "space", CY - 1),
    ]
    got, own_part = lax.optimization_barrier((got, own_part))
    sizes = [piece[0].size for piece in got]
    joined = jnp.concatenate([piece.reshape(width_in, -1) for piece in got], axis=1)
    lower_all, upper_all = swap(joined)
    offsets = [sum(sizes[:k]) for k in range(len(sizes) + 1)]

    def piece(joined_half, k):
        return joined_half[:, offsets[k] : offsets[k + 1]].reshape(got[k].shape)

    below, above = piece(lower_all, 0), piece(upper_all, 0)
    lower_row, upper_row = piece(lower_all, 1), piece(upper_all, 1)
    corner_ll, corner_hh = piece(lower_all, 2), piece(upper_all, 2)
    corner_lh, corner_hl = piece(lower_all, 3), piece(upper_all, 3)
    face_part = jnp.concatenate(
        [
            conv(below, weight[:1], ((0, 0), (1, 1), (1, 1))),
            conv(above, weight[2:], ((0, 0), (1, 1), (1, 1))),
        ],
        axis=1,
    )
    place_y = (lax.axis_index("space") + 4) % 8
    lower_rim = jnp.concatenate([corner_ll, lower_row, corner_hl], axis=1)
    upper_rim = jnp.concatenate([corner_lh, upper_row, corner_hh], axis=1)
    lower_rim = jnp.where(place_y > 0, lower_rim, jnp.zeros_like(lower_rim))
    upper_rim = jnp.where(place_y < 7, upper_rim, jnp.zeros_like(upper_rim))
    lower_part = conv(lower_rim, weight[:, :1], ((0, 0), (0, 0), (1, 1)))
    upper_part = conv(upper_rim, weight[:, 2:], ((0, 0), (0, 0), (1, 1)))
    width_out = own_part.shape[0]
    middle = jnp.zeros((width_out, size_x, size_y - 2, size_z), jnp.float32)
    rim_part = jnp.concatenate([lower_part, middle, upper_part], axis=2)
    total = (own_part + face_part + rim_part).reshape(width_out, -1)
    before = total + conv_bias[:, None]
    result = jnp.maximum(before, negative_slope * before)
    result = result.reshape(width_out, size_x, size_y * size_z).transpose(1, 0, 2)
    return result[None]


def solution(mesh):
    placed = (P("space", None, "chan", None), P(None, None, None, "chan", None), P("chan"))
    return jax.shard_map(
        body, mesh=mesh, in_specs=placed, out_specs=P("space", None, "chan", None), check_vma=False
    )
```

```python
import jax
import jax.numpy as jnp
from jax import lax
from jax.sharding import PartitionSpec as P

CY = 8


negative_slope = 0.3


def plain_shift(value, axis, steps):
    count = lax.axis_size(axis)
    return lax.ppermute(value, axis, [(source, (source + steps) % count) for source in range(count)])


def cross(lower_source, upper_source, axis, steps):
    count = lax.axis_size(axis)
    width = lax.axis_size("chan")
    run_y = width // 2
    pairs = []
    for source in range(count):
        for lane in range(width):
            place, core = divmod(lane, 2)
            target = (source + (steps if core == 0 else -steps)) % count
            crosses = (source // CY) % 2 != (target // CY) % 2
            moved = ((place + run_y // 2) % run_y) * 2 + core if crosses else lane
            pairs.append((source * width + lane, target * width + moved))
    on_first = lax.axis_index("chan") % 2 == 0
    sent = jnp.where(on_first, lower_source, upper_source)
    return lax.ppermute(sent, (axis, "chan"), pairs)


def swap(got):
    width = lax.axis_size("chan")
    on_first = lax.axis_index("chan") % 2 == 0
    swapped = lax.ppermute(got, "chan", [(lane, lane ^ 1) for lane in range(width)])
    return jnp.where(on_first, got, swapped), jnp.where(on_first, swapped, got)


def conv(field, taps, padding):
    return lax.conv_general_dilated(
        field[None],
        taps,
        window_strides=(1, 1, 1),
        padding=padding,
        dimension_numbers=("NCDHW", "DHWOI", "NCDHW"),
        preferred_element_type=jnp.float32,
    )[0]


def body(activation, weight, conv_bias):
    size_x = activation.shape[1]
    size_y = CY
    size_z = activation.shape[3] // size_y
    width = lax.axis_size("chan")
    own_block = activation[0].astype(jnp.bfloat16).reshape(-1, activation.shape[3])
    gathered = lax.all_gather(own_block, "chan", axis=0, tiled=True)
    gathered = gathered.reshape(width, size_x, -1, activation.shape[3]).transpose(0, 2, 1, 3)
    gathered = gathered.reshape(-1, size_x, size_y, size_z)
    own_part = conv(gathered, weight, ((1, 1), (1, 1), (1, 1)))
    spill_lo = conv(gathered[:, :1], weight[2:], ((0, 0), (2, 2), (1, 1)))
    spill_hi = conv(gathered[:, -1:], weight[:1], ((0, 0), (2, 2), (1, 1)))
    from_lo = plain_shift(spill_hi, "space", CY)
    from_hi = plain_shift(spill_lo, "space", -CY)
    row_lo = conv(gathered[:, :, :1], weight[:, 2:], ((1, 1), (0, 0), (1, 1)))
    row_hi = conv(gathered[:, :, -1:], weight[:, :1], ((1, 1), (0, 0), (1, 1)))
    from_lo, from_hi, own_part, row_lo, row_hi = lax.optimization_barrier((from_lo, from_hi, own_part, row_lo, row_hi))
    row_lo = row_lo + jnp.concatenate([from_lo[:, :, :1], from_hi[:, :, :1]], axis=1)
    row_hi = row_hi + jnp.concatenate([from_lo[:, :, -1:], from_hi[:, :, -1:]], axis=1)
    from_below = plain_shift(row_hi, "space", 1)
    from_above = plain_shift(row_lo, "space", -1)
    place_y = (lax.axis_index("space") + 4) % 8
    from_below = jnp.where(place_y > 0, from_below, jnp.zeros_like(from_below))
    from_above = jnp.where(place_y < 7, from_above, jnp.zeros_like(from_above))
    width_out = own_part.shape[0]
    x_part = jnp.concatenate([from_lo[:, :, 1:-1], from_hi[:, :, 1:-1]], axis=1)
    middle = jnp.zeros((width_out, size_x, size_y - 2, size_z), jnp.float32)
    y_part = jnp.concatenate([from_below, middle, from_above], axis=2)
    total = (own_part + x_part + y_part).reshape(width_out, -1)
    before = total + conv_bias[:, None]
    result = jnp.maximum(before, negative_slope * before)
    result = result.reshape(width_out, size_x, size_y * size_z).transpose(1, 0, 2)
    return result[None]


def solution(mesh):
    placed = (P("space", None, "chan", None), P(None, None, None, "chan", None), P("chan"))
    return jax.shard_map(
        body, mesh=mesh, in_specs=placed, out_specs=P("space", None, "chan", None), check_vma=False
    )
```

```python
import jax
import jax.numpy as jnp
from jax import lax
from jax.sharding import PartitionSpec as P

CY = 8


negative_slope = 0.3


def plain_shift(value, axis, steps):
    count = lax.axis_size(axis)
    return lax.ppermute(value, axis, [(source, (source + steps) % count) for source in range(count)])


def cross(lower_source, upper_source, axis, steps):
    count = lax.axis_size(axis)
    width = lax.axis_size("chan")
    run_y = width // 2
    pairs = []
    for source in range(count):
        for lane in range(width):
            place, core = divmod(lane, 2)
            target = (source + (steps if core == 0 else -steps)) % count
            crosses = (source // CY) % 2 != (target // CY) % 2
            moved = ((place + run_y // 2) % run_y) * 2 + core if crosses else lane
            pairs.append((source * width + lane, target * width + moved))
    on_first = lax.axis_index("chan") % 2 == 0
    sent = jnp.where(on_first, lower_source, upper_source)
    return lax.ppermute(sent, (axis, "chan"), pairs)


def swap(got):
    width = lax.axis_size("chan")
    on_first = lax.axis_index("chan") % 2 == 0
    swapped = lax.ppermute(got, "chan", [(lane, lane ^ 1) for lane in range(width)])
    return jnp.where(on_first, got, swapped), jnp.where(on_first, swapped, got)


def conv(field, taps, padding):
    return lax.conv_general_dilated(
        field[None],
        taps,
        window_strides=(1, 1, 1),
        padding=padding,
        dimension_numbers=("NCDHW", "DHWOI", "NCDHW"),
        preferred_element_type=jnp.float32,
    )[0]


def body(activation, weight, conv_bias):
    size_x = activation.shape[1]
    size_y = CY
    size_z = activation.shape[3] // size_y
    width = lax.axis_size("chan")
    own_block = activation[0].astype(jnp.bfloat16).reshape(-1, activation.shape[3])
    gathered = lax.all_gather(own_block, "chan", axis=0, tiled=True)
    gathered = gathered.reshape(width, size_x, -1, activation.shape[3]).transpose(0, 2, 1, 3)
    gathered = gathered.reshape(-1, size_x, size_y, size_z)
    own_part = conv(gathered, weight, ((1, 1), (1, 1), (1, 1)))
    row_lo = conv(gathered[:, :, :1], weight[:, 2:], ((2, 2), (0, 0), (1, 1)))
    row_hi = conv(gathered[:, :, -1:], weight[:, :1], ((2, 2), (0, 0), (1, 1)))
    from_below = plain_shift(row_hi, "space", 1)
    from_above = plain_shift(row_lo, "space", -1)
    spill_lo = conv(gathered[:, :1], weight[2:], ((0, 0), (1, 1), (1, 1)))
    spill_hi = conv(gathered[:, -1:], weight[:1], ((0, 0), (1, 1), (1, 1)))
    from_below, from_above, own_part, spill_lo, spill_hi = lax.optimization_barrier(
        (from_below, from_above, own_part, spill_lo, spill_hi)
    )
    place_y = (lax.axis_index("space") + 4) % 8
    from_below = jnp.where(place_y > 0, from_below, jnp.zeros_like(from_below))
    from_above = jnp.where(place_y < 7, from_above, jnp.zeros_like(from_above))
    width_out = own_part.shape[0]
    middle = jnp.zeros((width_out, 1, size_y - 2, size_z), jnp.float32)
    spill_lo = spill_lo + jnp.concatenate([from_below[:, :1], middle, from_above[:, :1]], axis=2)
    spill_hi = spill_hi + jnp.concatenate([from_below[:, -1:], middle, from_above[:, -1:]], axis=2)
    from_lo = plain_shift(spill_hi, "space", CY)
    from_hi = plain_shift(spill_lo, "space", -CY)
    x_part = jnp.concatenate([from_lo, from_hi], axis=1)
    middle = jnp.zeros((width_out, size_x, size_y - 2, size_z), jnp.float32)
    y_part = jnp.concatenate([from_below[:, 1:-1], middle, from_above[:, 1:-1]], axis=2)
    total = (own_part + x_part + y_part).reshape(width_out, -1)
    before = total + conv_bias[:, None]
    result = jnp.maximum(before, negative_slope * before)
    result = result.reshape(width_out, size_x, size_y * size_z).transpose(1, 0, 2)
    return result[None]


def solution(mesh):
    placed = (P("space", None, "chan", None), P(None, None, None, "chan", None), P("chan"))
    return jax.shard_map(
        body, mesh=mesh, in_specs=placed, out_specs=P("space", None, "chan", None), check_vma=False
    )
```

```python
import jax
import jax.numpy as jnp
from jax import lax
from jax.sharding import PartitionSpec as P

CY = 8


negative_slope = 0.3


def cross(lower_source, upper_source, axis, steps):
    count = lax.axis_size(axis)
    width = lax.axis_size("chan")
    run_y = width // 2
    pairs = []
    for source in range(count):
        for lane in range(width):
            place, core = divmod(lane, 2)
            target = (source + (steps if core == 0 else -steps)) % count
            crosses = (source // CY) % 2 != (target // CY) % 2
            moved = ((place + run_y // 2) % run_y) * 2 + core if crosses else lane
            pairs.append((source * width + lane, target * width + moved))
    on_first = lax.axis_index("chan") % 2 == 0
    sent = jnp.where(on_first, lower_source, upper_source)
    return lax.ppermute(sent, (axis, "chan"), pairs)


def swap(got):
    width = lax.axis_size("chan")
    on_first = lax.axis_index("chan") % 2 == 0
    swapped = lax.ppermute(got, "chan", [(lane, lane ^ 1) for lane in range(width)])
    return jnp.where(on_first, got, swapped), jnp.where(on_first, swapped, got)


def conv(field, taps, padding):
    return lax.conv_general_dilated(
        field[None],
        taps,
        window_strides=(1, 1, 1),
        padding=padding,
        dimension_numbers=("NCDHW", "DHWOI", "NCDHW"),
        preferred_element_type=jnp.float32,
    )[0]


def body(activation, weight, conv_bias):
    size_x = activation.shape[1]
    size_y = CY
    size_z = activation.shape[3] // size_y
    width = lax.axis_size("chan")
    own_block = activation[0].astype(jnp.bfloat16).reshape(-1, activation.shape[3])
    gathered = lax.all_gather(own_block, "chan", axis=0, tiled=True)
    gathered = gathered.reshape(width, size_x, -1, activation.shape[3]).transpose(0, 2, 1, 3)
    gathered = gathered.reshape(-1, size_x, size_y, size_z)
    own_part = conv(gathered, weight, ((1, 1), (1, 1), (1, 1)))
    width_in = gathered.shape[0]
    got = [
        cross(gathered[:, -1:], gathered[:, :1], "space", CY),
        cross(gathered[:, :, -1:], gathered[:, :, :1], "space", 1),
    ]
    corners_from, own_part = lax.optimization_barrier((gathered[:, ::size_x - 1, ::size_y - 1], own_part))
    got += [
        cross(corners_from[:, 1:, 1:], corners_from[:, :1, :1], "space", CY + 1),
        cross(corners_from[:, 1:, :1], corners_from[:, :1, 1:], "space", CY - 1),
    ]
    parity = lax.axis_index("chan") % 2
    mine_face = conv(
        got[0], lax.dynamic_slice_in_dim(weight, 2 * parity, 1, axis=0), ((0, 0), (1, 1), (1, 1))
    )
    got, own_part, mine_face = lax.optimization_barrier((got, own_part, mine_face))
    sizes = [piece[0].size for piece in got]
    joined = jnp.concatenate([piece.reshape(width_in, -1) for piece in got], axis=1)
    lower_all, upper_all = swap(joined)
    offsets = [sum(sizes[:k]) for k in range(len(sizes) + 1)]

    def piece(joined_half, k):
        return joined_half[:, offsets[k] : offsets[k + 1]].reshape(got[k].shape)

    below, above = piece(lower_all, 0), piece(upper_all, 0)
    lower_row, upper_row = piece(lower_all, 1), piece(upper_all, 1)
    corner_ll, corner_hh = piece(lower_all, 2), piece(upper_all, 2)
    corner_lh, corner_hl = piece(lower_all, 3), piece(upper_all, 3)
    on_first = parity == 0
    other_face = conv(
        jnp.where(on_first, above, below),
        lax.dynamic_slice_in_dim(weight, 2 - 2 * parity, 1, axis=0),
        ((0, 0), (1, 1), (1, 1)),
    )
    face_part = jnp.where(
        on_first,
        jnp.concatenate([mine_face, other_face], axis=1),
        jnp.concatenate([other_face, mine_face], axis=1),
    )
    place_y = (lax.axis_index("space") + 4) % 8
    lower_rim = jnp.concatenate([corner_ll, lower_row, corner_hl], axis=1)
    upper_rim = jnp.concatenate([corner_lh, upper_row, corner_hh], axis=1)
    lower_rim = jnp.where(place_y > 0, lower_rim, jnp.zeros_like(lower_rim))
    upper_rim = jnp.where(place_y < 7, upper_rim, jnp.zeros_like(upper_rim))
    lower_part = conv(lower_rim, weight[:, :1], ((0, 0), (0, 0), (1, 1)))
    upper_part = conv(upper_rim, weight[:, 2:], ((0, 0), (0, 0), (1, 1)))
    width_out = own_part.shape[0]
    middle = jnp.zeros((width_out, size_x, size_y - 2, size_z), jnp.float32)
    rim_part = jnp.concatenate([lower_part, middle, upper_part], axis=2)
    total = (own_part + face_part + rim_part).reshape(width_out, -1)
    before = total + conv_bias[:, None]
    result = jnp.maximum(before, negative_slope * before)
    result = result.reshape(width_out, size_x, size_y * size_z).transpose(1, 0, 2)
    return result[None]


def solution(mesh):
    placed = (P("space", None, "chan", None), P(None, None, None, "chan", None), P("chan"))
    return jax.shard_map(
        body, mesh=mesh, in_specs=placed, out_specs=P("space", None, "chan", None), check_vma=False
    )
```

```python
import jax
import jax.numpy as jnp
from jax import lax
from jax.sharding import PartitionSpec as P

CY = 8


negative_slope = 0.3


def cross(lower_source, upper_source, axis, steps):
    count = lax.axis_size(axis)
    width = lax.axis_size("chan")
    run_y = width // 2
    pairs = []
    for source in range(count):
        for lane in range(width):
            place, core = divmod(lane, 2)
            target = (source + (steps if core == 0 else -steps)) % count
            crosses = (source // CY) % 2 != (target // CY) % 2
            moved = ((place + run_y // 2) % run_y) * 2 + core if crosses else lane
            pairs.append((source * width + lane, target * width + moved))
    on_first = lax.axis_index("chan") % 2 == 0
    sent = jnp.where(on_first, lower_source, upper_source)
    return lax.ppermute(sent, (axis, "chan"), pairs)


def swap(got):
    width = lax.axis_size("chan")
    on_first = lax.axis_index("chan") % 2 == 0
    swapped = lax.ppermute(got, "chan", [(lane, lane ^ 1) for lane in range(width)])
    return jnp.where(on_first, got, swapped), jnp.where(on_first, swapped, got)


def conv(field, taps, padding):
    return lax.conv_general_dilated(
        field[None],
        taps,
        window_strides=(1, 1, 1),
        padding=padding,
        dimension_numbers=("NCDHW", "DHWOI", "NCDHW"),
        preferred_element_type=jnp.float32,
    )[0]


def body(activation, weight, conv_bias):
    size_x = activation.shape[1]
    size_y = CY
    size_z = activation.shape[3] // size_y
    width = lax.axis_size("chan")
    own_block = activation[0].astype(jnp.bfloat16).reshape(-1, activation.shape[3])
    gathered = lax.all_gather(own_block, "chan", axis=0, tiled=True)
    gathered = gathered.reshape(width, size_x, -1, activation.shape[3]).transpose(0, 2, 1, 3)
    gathered = gathered.reshape(-1, size_x, size_y, size_z)
    own_part = conv(gathered, weight, ((1, 1), (1, 1), (1, 1)))
    width_in = gathered.shape[0]
    got = [
        cross(gathered[:, -1:], gathered[:, :1], "space", CY),
        cross(gathered[:, :, -1:], gathered[:, :, :1], "space", 1),
    ]
    corners_from, own_part = lax.optimization_barrier((gathered[:, ::size_x - 1, ::size_y - 1], own_part))
    got += [
        cross(corners_from[:, 1:, 1:], corners_from[:, :1, :1], "space", CY + 1),
        cross(corners_from[:, 1:, :1], corners_from[:, :1, 1:], "space", CY - 1),
    ]
    parity = lax.axis_index("chan") % 2
    on_first = parity == 0
    width = lax.axis_size("chan")
    pairs_core = [(lane, lane ^ 1) for lane in range(width)]
    mine_face = conv(
        got[0], lax.dynamic_slice_in_dim(weight, 2 * parity, 1, axis=0), ((0, 0), (1, 1), (1, 1))
    )
    sizes = [piece[0].size for piece in got]
    early = jnp.concatenate([piece.reshape(width_in, -1) for piece in got[:2]], axis=1)
    early_other = lax.ppermute(early, "chan", pairs_core)
    face_other = early_other[:, : sizes[0]].reshape(got[0].shape)
    row_other = early_other[:, sizes[0] :].reshape(got[1].shape)
    other_face = conv(
        face_other, lax.dynamic_slice_in_dim(weight, 2 - 2 * parity, 1, axis=0), ((0, 0), (1, 1), (1, 1))
    )
    corners_got, own_part, mine_face, other_face, row_other = lax.optimization_barrier(
        (got[2:], own_part, mine_face, other_face, row_other)
    )
    late = jnp.concatenate([piece.reshape(width_in, -1) for piece in corners_got], axis=1)
    late_other = lax.ppermute(late, "chan", pairs_core)
    corner_a_other = late_other[:, : sizes[2]].reshape(got[2].shape)
    corner_b_other = late_other[:, sizes[2] :].reshape(got[3].shape)
    lower_row = jnp.where(on_first, got[1], row_other)
    upper_row = jnp.where(on_first, row_other, got[1])
    corner_ll = jnp.where(on_first, corners_got[0], corner_a_other)
    corner_hh = jnp.where(on_first, corner_a_other, corners_got[0])
    corner_lh = jnp.where(on_first, corners_got[1], corner_b_other)
    corner_hl = jnp.where(on_first, corner_b_other, corners_got[1])
    face_part = jnp.where(
        on_first,
        jnp.concatenate([mine_face, other_face], axis=1),
        jnp.concatenate([other_face, mine_face], axis=1),
    )
    place_y = (lax.axis_index("space") + 4) % 8
    lower_rim = jnp.concatenate([corner_ll, lower_row, corner_hl], axis=1)
    upper_rim = jnp.concatenate([corner_lh, upper_row, corner_hh], axis=1)
    lower_rim = jnp.where(place_y > 0, lower_rim, jnp.zeros_like(lower_rim))
    upper_rim = jnp.where(place_y < 7, upper_rim, jnp.zeros_like(upper_rim))
    lower_part = conv(lower_rim, weight[:, :1], ((0, 0), (0, 0), (1, 1)))
    upper_part = conv(upper_rim, weight[:, 2:], ((0, 0), (0, 0), (1, 1)))
    width_out = own_part.shape[0]
    middle = jnp.zeros((width_out, size_x, size_y - 2, size_z), jnp.float32)
    rim_part = jnp.concatenate([lower_part, middle, upper_part], axis=2)
    total = (own_part + face_part + rim_part).reshape(width_out, -1)
    before = total + conv_bias[:, None]
    result = jnp.maximum(before, negative_slope * before)
    result = result.reshape(width_out, size_x, size_y * size_z).transpose(1, 0, 2)
    return result[None]


def solution(mesh):
    placed = (P("space", None, "chan", None), P(None, None, None, "chan", None), P("chan"))
    return jax.shard_map(
        body, mesh=mesh, in_specs=placed, out_specs=P("space", None, "chan", None), check_vma=False
    )
```

```python
import jax
import jax.numpy as jnp
from jax import lax
from jax.sharding import PartitionSpec as P

CY = 8


negative_slope = 0.3


def cross(lower_source, upper_source, axis, steps):
    count = lax.axis_size(axis)
    width = lax.axis_size("chan")
    run_y = width // 2
    pairs = []
    for source in range(count):
        for lane in range(width):
            place, core = divmod(lane, 2)
            target = (source + (steps if core == 0 else -steps)) % count
            crosses = (source // CY) % 2 != (target // CY) % 2
            moved = ((place + run_y // 2) % run_y) * 2 + core if crosses else lane
            pairs.append((source * width + lane, target * width + moved))
    on_first = lax.axis_index("chan") % 2 == 0
    sent = jnp.where(on_first, lower_source, upper_source)
    return lax.ppermute(sent, (axis, "chan"), pairs)


def swap(got):
    width = lax.axis_size("chan")
    on_first = lax.axis_index("chan") % 2 == 0
    swapped = lax.ppermute(got, "chan", [(lane, lane ^ 1) for lane in range(width)])
    return jnp.where(on_first, got, swapped), jnp.where(on_first, swapped, got)


def conv(field, taps, padding):
    return lax.conv_general_dilated(
        field[None],
        taps,
        window_strides=(1, 1, 1),
        padding=padding,
        dimension_numbers=("NCDHW", "DHWOI", "NCDHW"),
        preferred_element_type=jnp.float32,
    )[0]


def body(activation, weight, conv_bias):
    size_x = activation.shape[1]
    size_y = CY
    size_z = activation.shape[3] // size_y
    width = lax.axis_size("chan")
    own_block = activation[0].astype(jnp.bfloat16).reshape(-1, activation.shape[3])
    gathered = lax.all_gather(own_block, "chan", axis=0, tiled=True)
    gathered = gathered.reshape(width, size_x, -1, activation.shape[3]).transpose(0, 2, 1, 3)
    gathered = gathered.reshape(-1, size_x, size_y, size_z)
    own_part = conv(gathered, weight, ((1, 1), (1, 1), (1, 1)))
    width_in = gathered.shape[0]
    got = [
        cross(gathered[:, -1:], gathered[:, :1], "space", CY),
        cross(gathered[:, :, -1:], gathered[:, :, :1], "space", 1),
    ]
    corners_from = gathered[:, ::size_x - 1, ::size_y - 1]
    got += [
        cross(corners_from[:, 1:, 1:], corners_from[:, :1, :1], "space", CY + 1),
        cross(corners_from[:, 1:, :1], corners_from[:, :1, 1:], "space", CY - 1),
    ]
    parity = lax.axis_index("chan") % 2
    on_first = parity == 0
    width = lax.axis_size("chan")
    pairs_core = [(lane, lane ^ 1) for lane in range(width)]
    faces_got, own_part = lax.optimization_barrier((got[:2], own_part))
    got = faces_got + got[2:]
    mine_face = conv(
        got[0], lax.dynamic_slice_in_dim(weight, 2 * parity, 1, axis=0), ((0, 0), (1, 1), (1, 1))
    )
    sizes = [piece[0].size for piece in got]
    early = jnp.concatenate([piece.reshape(width_in, -1) for piece in got[:2]], axis=1)
    early_other = lax.ppermute(early, "chan", pairs_core)
    face_other = early_other[:, : sizes[0]].reshape(got[0].shape)
    row_other = early_other[:, sizes[0] :].reshape(got[1].shape)
    other_face = conv(
        face_other, lax.dynamic_slice_in_dim(weight, 2 - 2 * parity, 1, axis=0), ((0, 0), (1, 1), (1, 1))
    )
    corners_got, own_part, mine_face, other_face, row_other = lax.optimization_barrier(
        (got[2:], own_part, mine_face, other_face, row_other)
    )
    late = jnp.concatenate([piece.reshape(width_in, -1) for piece in corners_got], axis=1)
    late_other = lax.ppermute(late, "chan", pairs_core)
    corner_a_other = late_other[:, : sizes[2]].reshape(got[2].shape)
    corner_b_other = late_other[:, sizes[2] :].reshape(got[3].shape)
    lower_row = jnp.where(on_first, got[1], row_other)
    upper_row = jnp.where(on_first, row_other, got[1])
    corner_ll = jnp.where(on_first, corners_got[0], corner_a_other)
    corner_hh = jnp.where(on_first, corner_a_other, corners_got[0])
    corner_lh = jnp.where(on_first, corners_got[1], corner_b_other)
    corner_hl = jnp.where(on_first, corner_b_other, corners_got[1])
    face_part = jnp.where(
        on_first,
        jnp.concatenate([mine_face, other_face], axis=1),
        jnp.concatenate([other_face, mine_face], axis=1),
    )
    place_y = (lax.axis_index("space") + 4) % 8
    lower_rim = jnp.concatenate([corner_ll, lower_row, corner_hl], axis=1)
    upper_rim = jnp.concatenate([corner_lh, upper_row, corner_hh], axis=1)
    lower_rim = jnp.where(place_y > 0, lower_rim, jnp.zeros_like(lower_rim))
    upper_rim = jnp.where(place_y < 7, upper_rim, jnp.zeros_like(upper_rim))
    lower_part = conv(lower_rim, weight[:, :1], ((0, 0), (0, 0), (1, 1)))
    upper_part = conv(upper_rim, weight[:, 2:], ((0, 0), (0, 0), (1, 1)))
    width_out = own_part.shape[0]
    middle = jnp.zeros((width_out, size_x, size_y - 2, size_z), jnp.float32)
    rim_part = jnp.concatenate([lower_part, middle, upper_part], axis=2)
    total = (own_part + face_part + rim_part).reshape(width_out, -1)
    before = total + conv_bias[:, None]
    result = jnp.maximum(before, negative_slope * before)
    result = result.reshape(width_out, size_x, size_y * size_z).transpose(1, 0, 2)
    return result[None]


def solution(mesh):
    placed = (P("space", None, "chan", None), P(None, None, None, "chan", None), P("chan"))
    return jax.shard_map(
        body, mesh=mesh, in_specs=placed, out_specs=P("space", None, "chan", None), check_vma=False
    )
```

```python
import jax
import jax.numpy as jnp
from jax import lax
from jax.sharding import PartitionSpec as P

CY = 8


negative_slope = 0.3


def cross(lower_source, upper_source, axis, steps):
    count = lax.axis_size(axis)
    width = lax.axis_size("chan")
    run_y = width // 2
    pairs = []
    for source in range(count):
        for lane in range(width):
            place, core = divmod(lane, 2)
            target = (source + (steps if core == 0 else -steps)) % count
            crosses = (source // CY) % 2 != (target // CY) % 2
            moved = ((place + run_y // 2) % run_y) * 2 + core if crosses else lane
            pairs.append((source * width + lane, target * width + moved))
    on_first = lax.axis_index("chan") % 2 == 0
    sent = jnp.where(on_first, lower_source, upper_source)
    return lax.ppermute(sent, (axis, "chan"), pairs)


def swap(got):
    width = lax.axis_size("chan")
    on_first = lax.axis_index("chan") % 2 == 0
    swapped = lax.ppermute(got, "chan", [(lane, lane ^ 1) for lane in range(width)])
    return jnp.where(on_first, got, swapped), jnp.where(on_first, swapped, got)


def conv(field, taps, padding):
    return lax.conv_general_dilated(
        field[None],
        taps,
        window_strides=(1, 1, 1),
        padding=padding,
        dimension_numbers=("NCDHW", "DHWOI", "NCDHW"),
        preferred_element_type=jnp.float32,
    )[0]


def body(activation, weight, conv_bias):
    size_x = activation.shape[1]
    size_y = CY
    size_z = activation.shape[3] // size_y
    own_block = activation[0].astype(jnp.bfloat16).transpose(1, 0, 2)
    gathered = lax.all_gather(own_block, "chan", axis=0, tiled=True)
    gathered = gathered.reshape(-1, size_x, size_y, size_z)
    own_part = conv(gathered, weight, ((1, 1), (1, 1), (1, 1)))
    width_in = gathered.shape[0]
    got = [
        cross(gathered[:, -1:], gathered[:, :1], "space", CY),
        cross(gathered[:, :, -1:], gathered[:, :, :1], "space", 1),
    ]
    corners_from, own_part = lax.optimization_barrier((gathered[:, ::size_x - 1, ::size_y - 1], own_part))
    got += [
        cross(corners_from[:, 1:, 1:], corners_from[:, :1, :1], "space", CY + 1),
        cross(corners_from[:, 1:, :1], corners_from[:, :1, 1:], "space", CY - 1),
    ]
    parity = lax.axis_index("chan") % 2
    on_first = parity == 0
    width = lax.axis_size("chan")
    pairs_core = [(lane, lane ^ 1) for lane in range(width)]
    mine_face = conv(
        got[0], lax.dynamic_slice_in_dim(weight, 2 * parity, 1, axis=0), ((0, 0), (1, 1), (1, 1))
    )
    sizes = [piece[0].size for piece in got]
    early = jnp.concatenate([piece.reshape(width_in, -1) for piece in got[:2]], axis=1)
    early_other = lax.ppermute(early, "chan", pairs_core)
    face_other = early_other[:, : sizes[0]].reshape(got[0].shape)
    row_other = early_other[:, sizes[0] :].reshape(got[1].shape)
    other_face = conv(
        face_other, lax.dynamic_slice_in_dim(weight, 2 - 2 * parity, 1, axis=0), ((0, 0), (1, 1), (1, 1))
    )
    corners_got, own_part, mine_face, other_face, row_other = lax.optimization_barrier(
        (got[2:], own_part, mine_face, other_face, row_other)
    )
    late = jnp.concatenate([piece.reshape(width_in, -1) for piece in corners_got], axis=1)
    late_other = lax.ppermute(late, "chan", pairs_core)
    corner_a_other = late_other[:, : sizes[2]].reshape(got[2].shape)
    corner_b_other = late_other[:, sizes[2] :].reshape(got[3].shape)
    lower_row = jnp.where(on_first, got[1], row_other)
    upper_row = jnp.where(on_first, row_other, got[1])
    corner_ll = jnp.where(on_first, corners_got[0], corner_a_other)
    corner_hh = jnp.where(on_first, corner_a_other, corners_got[0])
    corner_lh = jnp.where(on_first, corners_got[1], corner_b_other)
    corner_hl = jnp.where(on_first, corner_b_other, corners_got[1])
    face_part = jnp.where(
        on_first,
        jnp.concatenate([mine_face, other_face], axis=1),
        jnp.concatenate([other_face, mine_face], axis=1),
    )
    place_y = (lax.axis_index("space") + 4) % 8
    lower_rim = jnp.concatenate([corner_ll, lower_row, corner_hl], axis=1)
    upper_rim = jnp.concatenate([corner_lh, upper_row, corner_hh], axis=1)
    lower_rim = jnp.where(place_y > 0, lower_rim, jnp.zeros_like(lower_rim))
    upper_rim = jnp.where(place_y < 7, upper_rim, jnp.zeros_like(upper_rim))
    lower_part = conv(lower_rim, weight[:, :1], ((0, 0), (0, 0), (1, 1)))
    upper_part = conv(upper_rim, weight[:, 2:], ((0, 0), (0, 0), (1, 1)))
    width_out = own_part.shape[0]
    middle = jnp.zeros((width_out, size_x, size_y - 2, size_z), jnp.float32)
    rim_part = jnp.concatenate([lower_part, middle, upper_part], axis=2)
    total = (own_part + face_part + rim_part).reshape(width_out, -1)
    before = total + conv_bias[:, None]
    result = jnp.maximum(before, negative_slope * before)
    result = result.reshape(width_out, size_x, size_y * size_z).transpose(1, 0, 2)
    return result[None]


def solution(mesh):
    placed = (P("space", None, "chan", None), P(None, None, None, "chan", None), P("chan"))
    return jax.shard_map(
        body, mesh=mesh, in_specs=placed, out_specs=P("space", None, "chan", None), check_vma=False
    )
```

```python
import jax
import jax.numpy as jnp
from jax import lax
from jax.sharding import PartitionSpec as P

CY = 8


negative_slope = 0.3


def cross(lower_source, upper_source, axis, steps):
    count = lax.axis_size(axis)
    width = lax.axis_size("chan")
    run_y = width // 2
    pairs = []
    for source in range(count):
        for lane in range(width):
            place, core = divmod(lane, 2)
            target = (source + (steps if core == 0 else -steps)) % count
            crosses = (source // CY) % 2 != (target // CY) % 2
            moved = ((place + run_y // 2) % run_y) * 2 + core if crosses else lane
            pairs.append((source * width + lane, target * width + moved))
    on_first = lax.axis_index("chan") % 2 == 0
    sent = jnp.where(on_first, lower_source, upper_source)
    return lax.ppermute(sent, (axis, "chan"), pairs)


def swap(got):
    width = lax.axis_size("chan")
    on_first = lax.axis_index("chan") % 2 == 0
    swapped = lax.ppermute(got, "chan", [(lane, lane ^ 1) for lane in range(width)])
    return jnp.where(on_first, got, swapped), jnp.where(on_first, swapped, got)


def conv(field, taps, padding):
    return lax.conv_general_dilated(
        field[None],
        taps,
        window_strides=(1, 1, 1),
        padding=padding,
        dimension_numbers=("NCDHW", "DHWOI", "NCDHW"),
        preferred_element_type=jnp.float32,
    )[0]


def body(activation, weight, conv_bias):
    size_x = activation.shape[1]
    size_y = CY
    size_z = activation.shape[3] // size_y
    own_block = activation[0].astype(jnp.bfloat16).transpose(1, 0, 2)
    gathered = lax.all_gather(own_block, "chan", axis=0, tiled=True)
    gathered = gathered.reshape(-1, size_x, size_y, size_z)
    own_part = conv(gathered, weight, ((1, 1), (1, 1), (1, 1)))
    width_in = gathered.shape[0]
    got = [
        cross(gathered[:, -1:], gathered[:, :1], "space", CY),
        cross(gathered[:, :, -1:], gathered[:, :, :1], "space", 1),
    ]
    corners_from, own_part = lax.optimization_barrier((gathered[:, ::size_x - 1, ::size_y - 1], own_part))
    got += [
        cross(corners_from[:, 1:, 1:], corners_from[:, :1, :1], "space", CY + 1),
        cross(corners_from[:, 1:, :1], corners_from[:, :1, 1:], "space", CY - 1),
    ]
    parity = lax.axis_index("chan") % 2
    mine_face = conv(
        got[0], lax.dynamic_slice_in_dim(weight, 2 * parity, 1, axis=0), ((0, 0), (1, 1), (1, 1))
    )
    got, own_part, mine_face = lax.optimization_barrier((got, own_part, mine_face))
    sizes = [piece[0].size for piece in got]
    joined = jnp.concatenate([piece.reshape(width_in, -1) for piece in got], axis=1)
    lower_all, upper_all = swap(joined)
    offsets = [sum(sizes[:k]) for k in range(len(sizes) + 1)]

    def piece(joined_half, k):
        return joined_half[:, offsets[k] : offsets[k + 1]].reshape(got[k].shape)

    below, above = piece(lower_all, 0), piece(upper_all, 0)
    lower_row, upper_row = piece(lower_all, 1), piece(upper_all, 1)
    corner_ll, corner_hh = piece(lower_all, 2), piece(upper_all, 2)
    corner_lh, corner_hl = piece(lower_all, 3), piece(upper_all, 3)
    on_first = parity == 0
    other_face = conv(
        jnp.where(on_first, above, below),
        lax.dynamic_slice_in_dim(weight, 2 - 2 * parity, 1, axis=0),
        ((0, 0), (1, 1), (1, 1)),
    )
    face_part = jnp.where(
        on_first,
        jnp.concatenate([mine_face, other_face], axis=1),
        jnp.concatenate([other_face, mine_face], axis=1),
    )
    place_y = (lax.axis_index("space") + 4) % 8
    lower_rim = jnp.concatenate([corner_ll, lower_row, corner_hl], axis=1)
    upper_rim = jnp.concatenate([corner_lh, upper_row, corner_hh], axis=1)
    lower_rim = jnp.where(place_y > 0, lower_rim, jnp.zeros_like(lower_rim))
    upper_rim = jnp.where(place_y < 7, upper_rim, jnp.zeros_like(upper_rim))
    lower_part = conv(lower_rim, weight[:, :1], ((0, 0), (0, 0), (1, 1)))
    upper_part = conv(upper_rim, weight[:, 2:], ((0, 0), (0, 0), (1, 1)))
    width_out = own_part.shape[0]
    middle = jnp.zeros((width_out, size_x, size_y - 2, size_z), jnp.float32)
    rim_part = jnp.concatenate([lower_part, middle, upper_part], axis=2)
    total = (own_part + face_part + rim_part).reshape(width_out, -1)
    before = total + conv_bias[:, None]
    result = jnp.maximum(before, negative_slope * before)
    result = result.reshape(width_out, size_x, size_y * size_z).transpose(1, 0, 2)
    return result[None]


def solution(mesh):
    placed = (P("space", None, "chan", None), P(None, None, None, "chan", None), P("chan"))
    return jax.shard_map(
        body, mesh=mesh, in_specs=placed, out_specs=P("space", None, "chan", None), check_vma=False
    )
```

```python
import jax
import jax.numpy as jnp
from jax import lax
from jax.sharding import PartitionSpec as P

CY = 8


negative_slope = 0.3


def cross(lower_source, upper_source, axis, steps):
    count = lax.axis_size(axis)
    width = lax.axis_size("chan")
    run_y = width // 2
    pairs = []
    for source in range(count):
        for lane in range(width):
            place, core = divmod(lane, 2)
            target = (source + (steps if core == 0 else -steps)) % count
            crosses = (source // CY) % 2 != (target // CY) % 2
            moved = ((place + run_y // 2) % run_y) * 2 + core if crosses else lane
            pairs.append((source * width + lane, target * width + moved))
    on_first = lax.axis_index("chan") % 2 == 0
    sent = jnp.where(on_first, lower_source, upper_source)
    return lax.ppermute(sent, (axis, "chan"), pairs)


def swap(got):
    width = lax.axis_size("chan")
    on_first = lax.axis_index("chan") % 2 == 0
    swapped = lax.ppermute(got, "chan", [(lane, lane ^ 1) for lane in range(width)])
    return jnp.where(on_first, got, swapped), jnp.where(on_first, swapped, got)


def conv(field, taps, padding):
    return lax.conv_general_dilated(
        field[None],
        taps,
        window_strides=(1, 1, 1),
        padding=padding,
        dimension_numbers=("NCDHW", "DHWOI", "NDCHW"),
        preferred_element_type=jnp.float32,
    )[0]


def body(activation, weight, conv_bias):
    size_x = activation.shape[1]
    size_y = CY
    size_z = activation.shape[3] // size_y
    own_block = activation[0].astype(jnp.bfloat16).transpose(1, 0, 2)
    gathered = lax.all_gather(own_block, "chan", axis=0, tiled=True)
    gathered = gathered.reshape(-1, size_x, size_y, size_z)
    own_part = conv(gathered, weight, ((1, 1), (1, 1), (1, 1)))
    width_in = gathered.shape[0]
    got = [
        cross(gathered[:, -1:], gathered[:, :1], "space", CY),
        cross(gathered[:, :, -1:], gathered[:, :, :1], "space", 1),
    ]
    corners_from, own_part = lax.optimization_barrier((gathered[:, ::size_x - 1, ::size_y - 1], own_part))
    got += [
        cross(corners_from[:, 1:, 1:], corners_from[:, :1, :1], "space", CY + 1),
        cross(corners_from[:, 1:, :1], corners_from[:, :1, 1:], "space", CY - 1),
    ]
    parity = lax.axis_index("chan") % 2
    on_first = parity == 0
    width = lax.axis_size("chan")
    pairs_core = [(lane, lane ^ 1) for lane in range(width)]
    mine_face = conv(
        got[0], lax.dynamic_slice_in_dim(weight, 2 * parity, 1, axis=0), ((0, 0), (1, 1), (1, 1))
    )
    sizes = [piece[0].size for piece in got]
    early = jnp.concatenate([piece.reshape(width_in, -1) for piece in got[:2]], axis=1)
    early_other = lax.ppermute(early, "chan", pairs_core)
    face_other = early_other[:, : sizes[0]].reshape(got[0].shape)
    row_other = early_other[:, sizes[0] :].reshape(got[1].shape)
    other_face = conv(
        face_other, lax.dynamic_slice_in_dim(weight, 2 - 2 * parity, 1, axis=0), ((0, 0), (1, 1), (1, 1))
    )
    corners_got, own_part, mine_face, other_face, row_other = lax.optimization_barrier(
        (got[2:], own_part, mine_face, other_face, row_other)
    )
    late = jnp.concatenate([piece.reshape(width_in, -1) for piece in corners_got], axis=1)
    late_other = lax.ppermute(late, "chan", pairs_core)
    corner_a_other = late_other[:, : sizes[2]].reshape(got[2].shape)
    corner_b_other = late_other[:, sizes[2] :].reshape(got[3].shape)
    lower_row = jnp.where(on_first, got[1], row_other)
    upper_row = jnp.where(on_first, row_other, got[1])
    corner_ll = jnp.where(on_first, corners_got[0], corner_a_other)
    corner_hh = jnp.where(on_first, corner_a_other, corners_got[0])
    corner_lh = jnp.where(on_first, corners_got[1], corner_b_other)
    corner_hl = jnp.where(on_first, corner_b_other, corners_got[1])
    face_part = jnp.where(
        on_first,
        jnp.concatenate([mine_face, other_face], axis=0),
        jnp.concatenate([other_face, mine_face], axis=0),
    )
    place_y = (lax.axis_index("space") + 4) % 8
    lower_rim = jnp.concatenate([corner_ll, lower_row, corner_hl], axis=1)
    upper_rim = jnp.concatenate([corner_lh, upper_row, corner_hh], axis=1)
    lower_rim = jnp.where(place_y > 0, lower_rim, jnp.zeros_like(lower_rim))
    upper_rim = jnp.where(place_y < 7, upper_rim, jnp.zeros_like(upper_rim))
    lower_part = conv(lower_rim, weight[:, :1], ((0, 0), (0, 0), (1, 1)))
    upper_part = conv(upper_rim, weight[:, 2:], ((0, 0), (0, 0), (1, 1)))
    width_out = own_part.shape[1]
    middle = jnp.zeros((size_x, width_out, size_y - 2, size_z), jnp.float32)
    rim_part = jnp.concatenate([lower_part, middle, upper_part], axis=2)
    before = own_part + face_part + rim_part + conv_bias[None, :, None, None]
    result = jnp.maximum(before, negative_slope * before)
    return result.reshape(1, size_x, width_out, size_y * size_z)


def solution(mesh):
    placed = (P("space", None, "chan", None), P(None, None, None, "chan", None), P("chan"))
    return jax.shard_map(
        body, mesh=mesh, in_specs=placed, out_specs=P("space", None, "chan", None), check_vma=False
    )
```

```python
import jax
import jax.numpy as jnp
from jax import lax
from jax.sharding import PartitionSpec as P

CY = 8


negative_slope = 0.3


def cross(lower_source, upper_source, axis, steps, route=True):
    count = lax.axis_size(axis)
    width = lax.axis_size("chan")
    run_y = width // 2
    pairs = []
    for source in range(count):
        for lane in range(width):
            place, core = divmod(lane, 2)
            target = (source + (steps if core == 0 else -steps)) % count
            crosses = (source // CY) % 2 != (target // CY) % 2
            moved = ((place + run_y // 2) % run_y) * 2 + core if crosses and route else lane
            pairs.append((source * width + lane, target * width + moved))
    on_first = lax.axis_index("chan") % 2 == 0
    sent = jnp.where(on_first, lower_source, upper_source)
    return lax.ppermute(sent, (axis, "chan"), pairs)


def swap(got):
    width = lax.axis_size("chan")
    on_first = lax.axis_index("chan") % 2 == 0
    swapped = lax.ppermute(got, "chan", [(lane, lane ^ 1) for lane in range(width)])
    return jnp.where(on_first, got, swapped), jnp.where(on_first, swapped, got)


def conv(field, taps, padding):
    return lax.conv_general_dilated(
        field[None],
        taps,
        window_strides=(1, 1, 1),
        padding=padding,
        dimension_numbers=("NCDHW", "DHWOI", "NDCHW"),
        preferred_element_type=jnp.float32,
    )[0]


def body(activation, weight, conv_bias):
    size_x = activation.shape[1]
    size_y = CY
    size_z = activation.shape[3] // size_y
    own_block = activation[0].astype(jnp.bfloat16).transpose(1, 0, 2)
    gathered = lax.all_gather(own_block, "chan", axis=0, tiled=True)
    gathered = gathered.reshape(-1, size_x, size_y, size_z)
    own_part = conv(gathered, weight, ((1, 1), (1, 1), (1, 1)))
    width_in = gathered.shape[0]
    got = [
        cross(gathered[:, -1:], gathered[:, :1], "space", CY),
        cross(gathered[:, :, -1:], gathered[:, :, :1], "space", 1),
    ]
    corners_from, own_part = lax.optimization_barrier((gathered[:, ::size_x - 1, ::size_y - 1], own_part))
    got += [
        cross(corners_from[:, 1:, 1:], corners_from[:, :1, :1], "space", CY + 1, route=False),
        cross(corners_from[:, 1:, :1], corners_from[:, :1, 1:], "space", CY - 1, route=False),
    ]
    parity = lax.axis_index("chan") % 2
    on_first = parity == 0
    width = lax.axis_size("chan")
    pairs_core = [(lane, lane ^ 1) for lane in range(width)]
    mine_face = conv(
        got[0], lax.dynamic_slice_in_dim(weight, 2 * parity, 1, axis=0), ((0, 0), (1, 1), (1, 1))
    )
    sizes = [piece[0].size for piece in got]
    early = jnp.concatenate([piece.reshape(width_in, -1) for piece in got[:2]], axis=1)
    early_other = lax.ppermute(early, "chan", pairs_core)
    face_other = early_other[:, : sizes[0]].reshape(got[0].shape)
    row_other = early_other[:, sizes[0] :].reshape(got[1].shape)
    other_face = conv(
        face_other, lax.dynamic_slice_in_dim(weight, 2 - 2 * parity, 1, axis=0), ((0, 0), (1, 1), (1, 1))
    )
    corners_got, own_part, mine_face, other_face, row_other = lax.optimization_barrier(
        (got[2:], own_part, mine_face, other_face, row_other)
    )
    late = jnp.concatenate([piece.reshape(width_in, -1) for piece in corners_got], axis=1)
    late_other = lax.ppermute(late, "chan", pairs_core)
    corner_a_other = late_other[:, : sizes[2]].reshape(got[2].shape)
    corner_b_other = late_other[:, sizes[2] :].reshape(got[3].shape)
    lower_row = jnp.where(on_first, got[1], row_other)
    upper_row = jnp.where(on_first, row_other, got[1])
    corner_ll = jnp.where(on_first, corners_got[0], corner_a_other)
    corner_hh = jnp.where(on_first, corner_a_other, corners_got[0])
    corner_lh = jnp.where(on_first, corners_got[1], corner_b_other)
    corner_hl = jnp.where(on_first, corner_b_other, corners_got[1])
    face_part = jnp.where(
        on_first,
        jnp.concatenate([mine_face, other_face], axis=0),
        jnp.concatenate([other_face, mine_face], axis=0),
    )
    place_y = (lax.axis_index("space") + 4) % 8
    lower_rim = jnp.concatenate([corner_ll, lower_row, corner_hl], axis=1)
    upper_rim = jnp.concatenate([corner_lh, upper_row, corner_hh], axis=1)
    lower_rim = jnp.where(place_y > 0, lower_rim, jnp.zeros_like(lower_rim))
    upper_rim = jnp.where(place_y < 7, upper_rim, jnp.zeros_like(upper_rim))
    lower_part = conv(lower_rim, weight[:, :1], ((0, 0), (0, 0), (1, 1)))
    upper_part = conv(upper_rim, weight[:, 2:], ((0, 0), (0, 0), (1, 1)))
    width_out = own_part.shape[1]
    middle = jnp.zeros((size_x, width_out, size_y - 2, size_z), jnp.float32)
    rim_part = jnp.concatenate([lower_part, middle, upper_part], axis=2)
    before = own_part + face_part + rim_part + conv_bias[None, :, None, None]
    result = jnp.maximum(before, negative_slope * before)
    return result.reshape(1, size_x, width_out, size_y * size_z)


def solution(mesh):
    placed = (P("space", None, "chan", None), P(None, None, None, "chan", None), P("chan"))
    return jax.shard_map(
        body, mesh=mesh, in_specs=placed, out_specs=P("space", None, "chan", None), check_vma=False
    )
```

```python
import jax
import jax.numpy as jnp
from jax import lax
from jax.sharding import PartitionSpec as P

CY = 8


negative_slope = 0.3


def cross(lower_source, upper_source, axis, steps, shift=None):
    count = lax.axis_size(axis)
    width = lax.axis_size("chan")
    run_y = width // 2
    pairs = []
    for source in range(count):
        for lane in range(width):
            place, core = divmod(lane, 2)
            target = (source + (steps if core == 0 else -steps)) % count
            crosses = (source // CY) % 2 != (target // CY) % 2
            step_y = run_y // 2 if shift is None else shift
            moved = ((place + step_y) % run_y) * 2 + core if crosses else lane
            pairs.append((source * width + lane, target * width + moved))
    on_first = lax.axis_index("chan") % 2 == 0
    sent = jnp.where(on_first, lower_source, upper_source)
    return lax.ppermute(sent, (axis, "chan"), pairs)


def swap(got):
    width = lax.axis_size("chan")
    on_first = lax.axis_index("chan") % 2 == 0
    swapped = lax.ppermute(got, "chan", [(lane, lane ^ 1) for lane in range(width)])
    return jnp.where(on_first, got, swapped), jnp.where(on_first, swapped, got)


def conv(field, taps, padding):
    return lax.conv_general_dilated(
        field[None],
        taps,
        window_strides=(1, 1, 1),
        padding=padding,
        dimension_numbers=("NCDHW", "DHWOI", "NDCHW"),
        preferred_element_type=jnp.float32,
    )[0]


def body(activation, weight, conv_bias):
    size_x = activation.shape[1]
    size_y = CY
    size_z = activation.shape[3] // size_y
    own_block = activation[0].astype(jnp.bfloat16).transpose(1, 0, 2)
    gathered = lax.all_gather(own_block, "chan", axis=0, tiled=True)
    gathered = gathered.reshape(-1, size_x, size_y, size_z)
    own_part = conv(gathered, weight, ((1, 1), (1, 1), (1, 1)))
    width_in = gathered.shape[0]
    got = [
        cross(gathered[:, -1:], gathered[:, :1], "space", CY),
        cross(gathered[:, :, -1:], gathered[:, :, :1], "space", 1, shift=1),
    ]
    corners_from, own_part = lax.optimization_barrier((gathered[:, ::size_x - 1, ::size_y - 1], own_part))
    got += [
        cross(corners_from[:, 1:, 1:], corners_from[:, :1, :1], "space", CY + 1),
        cross(corners_from[:, 1:, :1], corners_from[:, :1, 1:], "space", CY - 1),
    ]
    parity = lax.axis_index("chan") % 2
    on_first = parity == 0
    width = lax.axis_size("chan")
    pairs_core = [(lane, lane ^ 1) for lane in range(width)]
    mine_face = conv(
        got[0], lax.dynamic_slice_in_dim(weight, 2 * parity, 1, axis=0), ((0, 0), (1, 1), (1, 1))
    )
    sizes = [piece[0].size for piece in got]
    early = jnp.concatenate([piece.reshape(width_in, -1) for piece in got[:2]], axis=1)
    early_other = lax.ppermute(early, "chan", pairs_core)
    face_other = early_other[:, : sizes[0]].reshape(got[0].shape)
    row_other = early_other[:, sizes[0] :].reshape(got[1].shape)
    other_face = conv(
        face_other, lax.dynamic_slice_in_dim(weight, 2 - 2 * parity, 1, axis=0), ((0, 0), (1, 1), (1, 1))
    )
    corners_got, own_part, mine_face, other_face, row_other = lax.optimization_barrier(
        (got[2:], own_part, mine_face, other_face, row_other)
    )
    late = jnp.concatenate([piece.reshape(width_in, -1) for piece in corners_got], axis=1)
    late_other = lax.ppermute(late, "chan", pairs_core)
    corner_a_other = late_other[:, : sizes[2]].reshape(got[2].shape)
    corner_b_other = late_other[:, sizes[2] :].reshape(got[3].shape)
    lower_row = jnp.where(on_first, got[1], row_other)
    upper_row = jnp.where(on_first, row_other, got[1])
    corner_ll = jnp.where(on_first, corners_got[0], corner_a_other)
    corner_hh = jnp.where(on_first, corner_a_other, corners_got[0])
    corner_lh = jnp.where(on_first, corners_got[1], corner_b_other)
    corner_hl = jnp.where(on_first, corner_b_other, corners_got[1])
    face_part = jnp.where(
        on_first,
        jnp.concatenate([mine_face, other_face], axis=0),
        jnp.concatenate([other_face, mine_face], axis=0),
    )
    place_y = (lax.axis_index("space") + 4) % 8
    lower_rim = jnp.concatenate([corner_ll, lower_row, corner_hl], axis=1)
    upper_rim = jnp.concatenate([corner_lh, upper_row, corner_hh], axis=1)
    lower_rim = jnp.where(place_y > 0, lower_rim, jnp.zeros_like(lower_rim))
    upper_rim = jnp.where(place_y < 7, upper_rim, jnp.zeros_like(upper_rim))
    lower_part = conv(lower_rim, weight[:, :1], ((0, 0), (0, 0), (1, 1)))
    upper_part = conv(upper_rim, weight[:, 2:], ((0, 0), (0, 0), (1, 1)))
    width_out = own_part.shape[1]
    middle = jnp.zeros((size_x, width_out, size_y - 2, size_z), jnp.float32)
    rim_part = jnp.concatenate([lower_part, middle, upper_part], axis=2)
    before = own_part + face_part + rim_part + conv_bias[None, :, None, None]
    result = jnp.maximum(before, negative_slope * before)
    return result.reshape(1, size_x, width_out, size_y * size_z)


def solution(mesh):
    placed = (P("space", None, "chan", None), P(None, None, None, "chan", None), P("chan"))
    return jax.shard_map(
        body, mesh=mesh, in_specs=placed, out_specs=P("space", None, "chan", None), check_vma=False
    )
```

```python
import jax
import jax.numpy as jnp
from jax import lax
from jax.sharding import PartitionSpec as P

CY = 8


negative_slope = 0.3


def cross(lower_source, upper_source, axis, steps, shift=None):
    count = lax.axis_size(axis)
    width = lax.axis_size("chan")
    run_y = width // 2
    pairs = []
    for source in range(count):
        for lane in range(width):
            place, core = divmod(lane, 2)
            target = (source + (steps if core == 0 else -steps)) % count
            crosses = (source // CY) % 2 != (target // CY) % 2
            step_y = run_y // 2 if shift is None else shift
            moved = ((place + step_y) % run_y) * 2 + core if crosses else lane
            pairs.append((source * width + lane, target * width + moved))
    on_first = lax.axis_index("chan") % 2 == 0
    sent = jnp.where(on_first, lower_source, upper_source)
    return lax.ppermute(sent, (axis, "chan"), pairs)


def swap(got):
    width = lax.axis_size("chan")
    on_first = lax.axis_index("chan") % 2 == 0
    swapped = lax.ppermute(got, "chan", [(lane, lane ^ 1) for lane in range(width)])
    return jnp.where(on_first, got, swapped), jnp.where(on_first, swapped, got)


def conv(field, taps, padding):
    return lax.conv_general_dilated(
        field[None],
        taps,
        window_strides=(1, 1, 1),
        padding=padding,
        dimension_numbers=("NCDHW", "DHWOI", "NDCHW"),
        preferred_element_type=jnp.float32,
    )[0]


def body(activation, weight, conv_bias):
    size_x = activation.shape[1]
    size_y = CY
    size_z = activation.shape[3] // size_y
    own_block = activation[0].astype(jnp.bfloat16).transpose(1, 0, 2)
    gathered = lax.all_gather(own_block, "chan", axis=0, tiled=True)
    gathered = gathered.reshape(-1, size_x, size_y, size_z)
    own_part = conv(gathered, weight, ((1, 1), (1, 1), (1, 1)))
    width_in = gathered.shape[0]
    got = [
        cross(gathered[:, -1:], gathered[:, :1], "space", CY, shift=3),
        cross(gathered[:, :, -1:], gathered[:, :, :1], "space", 1),
    ]
    corners_from, own_part = lax.optimization_barrier((gathered[:, ::size_x - 1, ::size_y - 1], own_part))
    got += [
        cross(corners_from[:, 1:, 1:], corners_from[:, :1, :1], "space", CY + 1),
        cross(corners_from[:, 1:, :1], corners_from[:, :1, 1:], "space", CY - 1),
    ]
    parity = lax.axis_index("chan") % 2
    on_first = parity == 0
    width = lax.axis_size("chan")
    pairs_core = [(lane, lane ^ 1) for lane in range(width)]
    mine_face = conv(
        got[0], lax.dynamic_slice_in_dim(weight, 2 * parity, 1, axis=0), ((0, 0), (1, 1), (1, 1))
    )
    sizes = [piece[0].size for piece in got]
    early = jnp.concatenate([piece.reshape(width_in, -1) for piece in got[:2]], axis=1)
    early_other = lax.ppermute(early, "chan", pairs_core)
    face_other = early_other[:, : sizes[0]].reshape(got[0].shape)
    row_other = early_other[:, sizes[0] :].reshape(got[1].shape)
    other_face = conv(
        face_other, lax.dynamic_slice_in_dim(weight, 2 - 2 * parity, 1, axis=0), ((0, 0), (1, 1), (1, 1))
    )
    corners_got, own_part, mine_face, other_face, row_other = lax.optimization_barrier(
        (got[2:], own_part, mine_face, other_face, row_other)
    )
    late = jnp.concatenate([piece.reshape(width_in, -1) for piece in corners_got], axis=1)
    late_other = lax.ppermute(late, "chan", pairs_core)
    corner_a_other = late_other[:, : sizes[2]].reshape(got[2].shape)
    corner_b_other = late_other[:, sizes[2] :].reshape(got[3].shape)
    lower_row = jnp.where(on_first, got[1], row_other)
    upper_row = jnp.where(on_first, row_other, got[1])
    corner_ll = jnp.where(on_first, corners_got[0], corner_a_other)
    corner_hh = jnp.where(on_first, corner_a_other, corners_got[0])
    corner_lh = jnp.where(on_first, corners_got[1], corner_b_other)
    corner_hl = jnp.where(on_first, corner_b_other, corners_got[1])
    face_part = jnp.where(
        on_first,
        jnp.concatenate([mine_face, other_face], axis=0),
        jnp.concatenate([other_face, mine_face], axis=0),
    )
    place_y = (lax.axis_index("space") + 4) % 8
    lower_rim = jnp.concatenate([corner_ll, lower_row, corner_hl], axis=1)
    upper_rim = jnp.concatenate([corner_lh, upper_row, corner_hh], axis=1)
    lower_rim = jnp.where(place_y > 0, lower_rim, jnp.zeros_like(lower_rim))
    upper_rim = jnp.where(place_y < 7, upper_rim, jnp.zeros_like(upper_rim))
    lower_part = conv(lower_rim, weight[:, :1], ((0, 0), (0, 0), (1, 1)))
    upper_part = conv(upper_rim, weight[:, 2:], ((0, 0), (0, 0), (1, 1)))
    width_out = own_part.shape[1]
    middle = jnp.zeros((size_x, width_out, size_y - 2, size_z), jnp.float32)
    rim_part = jnp.concatenate([lower_part, middle, upper_part], axis=2)
    before = own_part + face_part + rim_part + conv_bias[None, :, None, None]
    result = jnp.maximum(before, negative_slope * before)
    return result.reshape(1, size_x, width_out, size_y * size_z)


def solution(mesh):
    placed = (P("space", None, "chan", None), P(None, None, None, "chan", None), P("chan"))
    return jax.shard_map(
        body, mesh=mesh, in_specs=placed, out_specs=P("space", None, "chan", None), check_vma=False
    )
```
